32 devices in a mesh: grp: 8 (over y, x, core), mem: 4 (over z).
Axes of the slice: x: 2, y: 2, z: 4, core: 2. Of those that a mesh axis runs over, the one named last changes fastest.
Arguments:
- points: float32 [16, 32768], P(None, ('grp', 'mem')), may hold values from -6 to 6
- residual: float32 [16, 32768], P(None, ('grp', 'mem')), may hold values from -6 to 6
- coef: float32 [16, 32768], P(None, ('grp', 'mem')), may hold values from -3 to 3
- block_of: int32 [32768], P(('grp', 'mem')), may hold values from 0 to 7, as said below
- order: int32 [2], replicated, may hold values from 0 to 7
- inverse: float32 [8, 4096, 4096], P('grp', 'mem'), may hold values from -1 to 2
Outputs:
- residual_out: float32 [16, 32768], P(None, ('grp', 'mem'))
- coef_out: float32 [16, 32768], P(None, ('grp', 'mem'))
The draws below stay inside these ranges and needn't reach their ends.
Inputs may be any that keep to these rules, and one draw needn't show every extreme that they name: `block_of`: each run of 1024 consecutive points (the points of one device) holds exactly 128 points of every block.
All inputs are finite; a program needn't handle non-finite values.
Results may differ from the reference program's by a relative error of at most 0.00013.
Values sent between devices are 32-bit elements; how exact they have to be, the bound alone decides.
No kernel may reach another device: no remote copies, remote signals or barrier semaphores. Data moves between devices by JAX's collectives and lax.ppermute only.
A program may use at most 128 MiB of HBM per device.

```python
import math
import jax
import jax.numpy as jnp
from jax import lax

FEAT = 16
RHS = 16
B = 4096
STEPS = 2
NBLK = 8
ROWS = 1024
PER_DEV = 128
N = 32768
N_GRP = 8
N_MEM = 4


def draw_block_of(key, part):
    base = jnp.tile(jnp.arange(NBLK, dtype=jnp.int32), PER_DEV)
    subkeys = jax.random.split(jax.random.fold_in(key, 11), N // ROWS)
    shuffled = jax.vmap(lambda subkey: jax.random.permutation(subkey, base))(subkeys)
    return shuffled.reshape(-1).astype(jnp.int32)


def draw_inverse(key, part):
    first, second = jax.random.split(jax.random.fold_in(key, 23))
    diagonal = jnp.exp(jax.random.uniform(first, (NBLK, B), jnp.float32, math.log(0.3), math.log(1.0)))
    offdiag = jax.random.normal(second, (NBLK, B, B), jnp.float32) * (0.3 / math.sqrt(B))
    identity = jnp.eye(B, dtype=jnp.float32)
    return offdiag + identity[None, :, :] * diagonal[:, :, None]


def block_scale(key, extent, cuts, smallest, largest):
    def one(dim, shards_of):
        draws = jax.random.uniform(jax.random.fold_in(jax.random.fold_in(key, 6), dim), (shards_of,), jnp.float32, smallest / len(cuts), largest / len(cuts))
        return jnp.repeat(jnp.exp(draws), extent[dim] // shards_of).reshape((-1,) + (1,) * (len(extent) - dim - 1))

    factor_of = one(*cuts[0])
    for cut in cuts[1:]:
        factor_of = factor_of * one(*cut)
    return factor_of


def scatter_about(rng, extent, width, bound, cuts=(), kind=jnp.bfloat16):
    factor_of = block_scale(rng, extent, cuts, -0.22, 0.18) if cuts else 1.0
    array = jax.random.normal(rng, extent, jnp.float32) * width * factor_of
    return jnp.minimum(jnp.maximum(array, -bound), bound).astype(kind)


def setup_inputs(seed: int = 0) -> dict:
    keys = jax.random.split(jax.random.key(seed), 7)
    points = scatter_about(keys[0], (FEAT, N), 1.0, 6.0, ((1, 32),), jnp.float32)
    residual = scatter_about(keys[1], (RHS, N), 1.0, 6.0, ((1, 32),), jnp.float32)
    coef = scatter_about(keys[2], (RHS, N), 0.5, 3.0, ((1, 32),), jnp.float32)
    block_of = draw_block_of(jax.random.fold_in(keys[6], 71), 0)
    order = jax.random.randint(keys[4], (STEPS,), 0, NBLK).astype(jnp.int32)
    inverse = draw_inverse(jax.random.fold_in(keys[6], 71), 0)
    return {"points": points, "residual": residual, "coef": coef, "block_of": block_of, "order": order, "inverse": inverse}


ridge_weight = 0.5
kernel_scale = 0.125


def reference(points, residual, coef, block_of, order, inverse):
    total = points.shape[1]
    devices = N_GRP * N_MEM
    rows = total // devices
    per = B // devices
    hi = lax.Precision.HIGHEST
    for step_index in range(STEPS):
        block_id = order[step_index]
        inside = (block_of == block_id).reshape(devices, rows)
        position = jnp.cumsum(inside.astype(jnp.int32), axis=1) - 1
        ranks = (jnp.arange(devices, dtype=jnp.int32)[:, None] * per + position).astype(jnp.int32)
        target = jnp.where(inside, ranks, B).reshape(-1).astype(jnp.int32)
        members = jnp.zeros((B,), jnp.int32).at[target].set(jnp.arange(total, dtype=jnp.int32), mode="drop")
        chosen_res = residual[:, members]
        chosen_pts = points[:, members]
        matrix = lax.dynamic_index_in_dim(inverse, block_id, 0, keepdims=False)
        delta = lax.dot_general(chosen_res, matrix, (((1,), (1,)), ((), ())), precision=hi)
        norms_block = jnp.sum(chosen_pts * chosen_pts, axis=0)
        grouped = points.reshape(points.shape[0], total // B, B).transpose(1, 0, 2)

        def rowblock(local):
            norms_local = jnp.sum(local * local, axis=0)
            cross = lax.dot_general(local, chosen_pts, (((0,), (0,)), ((), ())), precision=hi)
            kernel = jnp.exp(-kernel_scale * (norms_local[:, None] + norms_block[None, :] - 2.0 * cross))
            return lax.dot_general(delta, kernel, (((1,), (1,)), ((), ())), precision=hi)

        update = lax.map(rowblock, grouped)
        update = update.transpose(1, 0, 2).reshape(residual.shape[0], total)
        residual = residual - update
        residual = residual.at[:, members].add(-ridge_weight * delta)
        coef = coef.at[:, members].add(delta)
    return residual, coef
```

```python
import jax
import jax.numpy as jnp
from jax import lax
from jax.sharding import PartitionSpec as P

B = 4096
STEPS = 2

ridge_weight = 0.5
kernel_scale = 0.125
ALL = ("grp", "mem")


def gather_all(piece, n_dev):
    sent = jnp.broadcast_to(piece[None], (n_dev,) + piece.shape)
    return lax.all_to_all(sent, ALL, 0, 0, tiled=True)


def body(points, residual, coef, block_of, order, inverse):
    highest = lax.Precision.HIGHEST
    high = lax.Precision.HIGH
    n_grp = lax.axis_size("grp")
    n_mem = lax.axis_size("mem")
    n_dev = n_grp * n_mem
    per = B // n_dev
    chunk = B // n_mem
    slots = inverse.shape[0]
    feat = points.shape[0]
    rhs = residual.shape[0]
    mine = lax.axis_index("grp") * n_mem + lax.axis_index("mem")
    norms_local = jnp.sum(points * points, axis=0)
    for step_index in range(STEPS):
        block_id = order[step_index]
        inside = block_of == block_id
        position = jnp.cumsum(inside.astype(jnp.int32)) - 1
        select = (
            (position[:, None] == jnp.arange(per, dtype=jnp.int32)[None, :]) & inside[:, None]
        ).astype(jnp.float32)
        chosen = jnp.dot(jnp.concatenate([residual, points], axis=0), select, precision=highest)
        gathered = gather_all(chosen, n_dev)
        gathered = jnp.transpose(gathered, (1, 0, 2)).reshape(rhs + feat, B)
        block_res = gathered[:rhs]
        block_pts = gathered[rhs:]
        matrix_rows = lax.dynamic_index_in_dim(inverse, block_id % slots, 0, keepdims=False)
        solved = lax.dot_general(
            block_res, matrix_rows, (((1,), (1,)), ((), ())), precision=high
        )
        owner = block_id // slots
        pieces = jnp.transpose(solved.reshape(rhs, n_grp, per), (1, 0, 2))
        scattered = lax.all_to_all(pieces, "grp", 0, 0, tiled=True)
        piece = lax.dynamic_index_in_dim(scattered, owner, 0, keepdims=False)
        pieces_all = gather_all(piece, n_dev)
        pieces_all = jnp.transpose(pieces_all.reshape(n_grp, n_mem, rhs, per), (2, 1, 0, 3))
        delta = pieces_all.reshape(rhs, B)
        norms_block = jnp.sum(block_pts * block_pts, axis=0)
        cross = lax.dot_general(points, block_pts, (((0,), (0,)), ((), ())), precision=highest)
        kernel = jnp.exp(
            -kernel_scale * (norms_local[:, None] + norms_block[None, :] - 2.0 * cross)
        )
        update = lax.dot_general(delta, kernel, (((1,), (1,)), ((), ())), precision=high)
        owned = lax.dynamic_slice_in_dim(delta, mine * per, per, axis=1)
        spread_back = lax.dot_general(owned, select, (((1,), (1,)), ((), ())), precision=highest)
        residual = residual - update - ridge_weight * spread_back
        coef = coef + spread_back
    return (residual, coef)


def solution(mesh):
    in_specs = (
        P(None, ("grp", "mem")),
        P(None, ("grp", "mem")),
        P(None, ("grp", "mem")),
        P(("grp", "mem")),
        P(),
        P("grp", "mem", None),
    )
    out_specs = (P(None, ("grp", "mem")), P(None, ("grp", "mem")))
    return jax.shard_map(body, mesh=mesh, in_specs=in_specs, out_specs=out_specs, check_vma=False)
```

```python
import jax
import jax.numpy as jnp
from jax import lax
from jax.sharding import PartitionSpec as P

B = 4096
STEPS = 2

ridge_weight = 0.5
kernel_scale = 0.125
ALL = ("grp", "mem")
HIGHEST = lax.Precision.HIGHEST
HIGH = lax.Precision.HIGH


def gather_all(piece, n_dev):
    sent = jnp.broadcast_to(piece[None], (n_dev,) + piece.shape)
    return lax.all_to_all(sent, ALL, 0, 0, tiled=True)


def split3(x):
    x1 = lax.reduce_precision(x, exponent_bits=8, mantissa_bits=7)
    r1 = x - x1
    x2 = lax.reduce_precision(r1, exponent_bits=8, mantissa_bits=7)
    r2 = r1 - x2
    return x1.astype(jnp.bfloat16), x2.astype(jnp.bfloat16), r2.astype(jnp.bfloat16)


def kern(u, v):
    nu = jnp.sum(u * u, axis=0, keepdims=True)
    nv = jnp.sum(v * v, axis=0, keepdims=True)
    u1, u2, u3 = split3(u)
    v1, v2, v3 = split3(-2.0 * v)
    a1, a2, a3 = split3(nu)
    b1, b2, b3 = split3(nv)
    one_u = jnp.ones_like(a1)
    one_v = jnp.ones_like(b1)
    left = jnp.concatenate([u1, u1, u2, u1, u3, u2, a1, a2, a3, one_u, one_u, one_u], axis=0)
    right = jnp.concatenate([v1, v2, v1, v3, v1, v2, one_v, one_v, one_v, b1, b2, b3], axis=0)
    dist = lax.dot_general(left, right, (((0,), (0,)), ((), ())), preferred_element_type=jnp.float32)
    return jnp.exp(-kernel_scale * dist)


def apply_kernel(delta, kernel):
    return lax.dot_general(delta, kernel, (((1,), (1,)), ((), ())), precision=HIGH)


def body(points, residual, coef, block_of, order, inverse):
    n_grp = lax.axis_size("grp")
    n_mem = lax.axis_size("mem")
    n_dev = n_grp * n_mem
    per = B // n_dev
    slots = inverse.shape[0]
    feat = points.shape[0]
    rhs = residual.shape[0]
    mine = lax.axis_index("grp") * n_mem + lax.axis_index("mem")

    def selector(block_id):
        inside = block_of == block_id
        position = jnp.cumsum(inside.astype(jnp.int32)) - 1
        return (
            (position[:, None] == jnp.arange(per, dtype=jnp.int32)[None, :]) & inside[:, None]
        ).astype(jnp.float32)

    def solve(block_res, block_id):
        matrix_rows = lax.dynamic_index_in_dim(inverse, block_id % slots, 0, keepdims=False)
        solved = lax.dot_general(
            block_res, matrix_rows, (((1,), (1,)), ((), ())), precision=HIGH
        )
        owner = block_id // slots
        pieces = jnp.transpose(solved.reshape(rhs, n_grp, per), (1, 0, 2))
        scattered = lax.all_to_all(pieces, "grp", 0, 0, tiled=True)
        piece = lax.dynamic_index_in_dim(scattered, owner, 0, keepdims=False)
        pieces_all = gather_all(piece, n_dev)
        pieces_all = jnp.transpose(pieces_all.reshape(n_grp, n_mem, rhs, per), (2, 1, 0, 3))
        return pieces_all.reshape(rhs, B)

    def to_block(gathered, rows):
        return jnp.transpose(gathered, (1, 0, 2)).reshape(rows, B)

    block0, block1 = order[0], order[1]
    sel0 = selector(block0)
    sel1 = selector(block1)
    chosen0 = jnp.dot(jnp.concatenate([residual, points], axis=0), sel0, precision=HIGHEST)
    chosen1 = jnp.dot(jnp.concatenate([residual, points], axis=0), sel1, precision=HIGHEST)
    res1_start = chosen1[:rhs]
    pts1_local = chosen1[rhs:]
    gathered = to_block(gather_all(jnp.concatenate([chosen0, pts1_local], axis=0), n_dev), rhs + 2 * feat)
    block_res0 = gathered[:rhs]
    block_pts0 = gathered[rhs:rhs + feat]
    block_pts1 = gathered[rhs + feat:]

    delta0 = solve(block_res0, block0)
    owned0 = lax.dynamic_slice_in_dim(delta0, mine * per, per, axis=1)
    early = apply_kernel(delta0, kern(pts1_local, block_pts0))
    overlap = jnp.dot(sel0.T, sel1, precision=HIGHEST)
    res1_local = res1_start - early - ridge_weight * jnp.dot(owned0, overlap, precision=HIGHEST)
    block_res1 = to_block(gather_all(res1_local, n_dev), rhs)

    spread0 = lax.dot_general(owned0, sel0, (((1,), (1,)), ((), ())), precision=HIGHEST)
    update0 = apply_kernel(delta0, kern(points, block_pts0))
    residual = residual - update0 - ridge_weight * spread0
    coef = coef + spread0
    kernel1 = kern(points, block_pts1)

    delta1 = solve(block_res1, block1)
    owned1 = lax.dynamic_slice_in_dim(delta1, mine * per, per, axis=1)
    spread1 = lax.dot_general(owned1, sel1, (((1,), (1,)), ((), ())), precision=HIGHEST)
    update1 = apply_kernel(delta1, kernel1)
    residual = residual - update1 - ridge_weight * spread1
    coef = coef + spread1
    return (residual, coef)


def solution(mesh):
    in_specs = (
        P(None, ("grp", "mem")),
        P(None, ("grp", "mem")),
        P(None, ("grp", "mem")),
        P(("grp", "mem")),
        P(),
        P("grp", "mem", None),
    )
    out_specs = (P(None, ("grp", "mem")), P(None, ("grp", "mem")))
    return jax.shard_map(body, mesh=mesh, in_specs=in_specs, out_specs=out_specs, check_vma=False)
```

```python
import jax
import jax.numpy as jnp
from jax import lax
from jax.sharding import PartitionSpec as P

B = 4096
STEPS = 2

ridge_weight = 0.5
kernel_scale = 0.125
ALL = ("grp", "mem")
HIGHEST = lax.Precision.HIGHEST
HIGH = lax.Precision.HIGH


def gather_all(piece, n_dev):
    sent = jnp.broadcast_to(piece[None], (n_dev,) + piece.shape)
    return lax.all_to_all(sent, ALL, 0, 0, tiled=True)


def split3(x):
    x1 = lax.reduce_precision(x, exponent_bits=8, mantissa_bits=7)
    r1 = x - x1
    x2 = lax.reduce_precision(r1, exponent_bits=8, mantissa_bits=7)
    r2 = r1 - x2
    return x1.astype(jnp.bfloat16), x2.astype(jnp.bfloat16), r2.astype(jnp.bfloat16)


def kern(u, v):
    nu = jnp.sum(u * u, axis=0, keepdims=True)
    nv = jnp.sum(v * v, axis=0, keepdims=True)
    u1, u2, u3 = split3(u)
    v1, v2, v3 = split3(-2.0 * v)
    a1, a2, a3 = split3(nu)
    b1, b2, b3 = split3(nv)
    one_u = jnp.ones_like(a1)
    one_v = jnp.ones_like(b1)
    left = jnp.concatenate([u1, u1, u2, u1, u3, u2, a1, a2, a3, one_u, one_u, one_u], axis=0)
    right = jnp.concatenate([v1, v2, v1, v3, v1, v2, one_v, one_v, one_v, b1, b2, b3], axis=0)
    dist = lax.dot_general(left, right, (((0,), (0,)), ((), ())), preferred_element_type=jnp.float32)
    kernel = jnp.exp(-kernel_scale * dist)
    k1 = lax.reduce_precision(kernel, exponent_bits=8, mantissa_bits=7)
    return k1.astype(jnp.bfloat16), (kernel - k1).astype(jnp.bfloat16)


def apply_kernel(delta, kernel):
    k1, k2 = kernel
    d1f = lax.reduce_precision(delta, exponent_bits=8, mantissa_bits=7)
    d1 = d1f.astype(jnp.bfloat16)
    d2 = (delta - d1f).astype(jnp.bfloat16)
    rows = delta.shape[0]
    dims = (((1,), (1,)), ((), ()))
    both = lax.dot_general(jnp.concatenate([d1, d2], axis=0), k1, dims, preferred_element_type=jnp.float32)
    low = lax.dot_general(d1, k2, dims, preferred_element_type=jnp.float32)
    return (both[:rows] + both[rows:]) + low


def exact_dot(x, onehot, dims):
    rows = x.shape[0]
    parts = jnp.concatenate(split3(x), axis=0)
    out = lax.dot_general(parts, onehot, dims, preferred_element_type=jnp.float32)
    return (out[:rows] + out[rows:2 * rows]) + out[2 * rows:]


def body(points, residual, coef, block_of, order, inverse):
    n_grp = lax.axis_size("grp")
    n_mem = lax.axis_size("mem")
    n_dev = n_grp * n_mem
    per = B // n_dev
    slots = inverse.shape[0]
    feat = points.shape[0]
    rhs = residual.shape[0]
    mine = lax.axis_index("grp") * n_mem + lax.axis_index("mem")

    def selector(block_id):
        inside = block_of == block_id
        position = jnp.cumsum(inside.astype(jnp.int32)) - 1
        return (
            (position[:, None] == jnp.arange(per, dtype=jnp.int32)[None, :]) & inside[:, None]
        ).astype(jnp.bfloat16)

    def solve(block_res, block_id):
        matrix_rows = lax.dynamic_index_in_dim(inverse, block_id % slots, 0, keepdims=False)
        solved = lax.dot_general(
            block_res, matrix_rows, (((1,), (1,)), ((), ())), precision=HIGH
        )
        owner = block_id // slots
        pieces = jnp.transpose(solved.reshape(rhs, n_grp, per), (1, 0, 2))
        scattered = lax.all_to_all(pieces, "grp", 0, 0, tiled=True)
        piece = lax.dynamic_index_in_dim(scattered, owner, 0, keepdims=False)
        pieces_all = gather_all(piece, n_dev)
        pieces_all = jnp.transpose(pieces_all.reshape(n_grp, n_mem, rhs, per), (2, 1, 0, 3))
        return pieces_all.reshape(rhs, B)

    def to_block(gathered, rows):
        return jnp.transpose(gathered, (1, 0, 2)).reshape(rows, B)

    block0, block1 = order[0], order[1]
    sel0 = selector(block0)
    sel1 = selector(block1)
    plain = (((1,), (0,)), ((), ()))
    chosen = exact_dot(
        jnp.concatenate([residual, points], axis=0), jnp.concatenate([sel0, sel1], axis=1), plain
    )
    chosen0 = chosen[:, :per]
    res1_start = chosen[:rhs, per:]
    pts1_local = chosen[rhs:, per:]
    gathered = to_block(gather_all(jnp.concatenate([chosen0, pts1_local], axis=0), n_dev), rhs + 2 * feat)
    block_res0 = gathered[:rhs]
    block_pts0 = gathered[rhs:rhs + feat]
    block_pts1 = gathered[rhs + feat:]

    delta0 = solve(block_res0, block0)
    owned0 = lax.dynamic_slice_in_dim(delta0, mine * per, per, axis=1)
    early = apply_kernel(delta0, kern(pts1_local, block_pts0))
    overlap = lax.dot_general(sel0, sel1, (((0,), (0,)), ((), ())), preferred_element_type=jnp.float32)
    overlap = overlap.astype(jnp.bfloat16)
    res1_local = res1_start - early - ridge_weight * exact_dot(owned0, overlap, plain)
    block_res1 = to_block(gather_all(res1_local, n_dev), rhs)

    spread0 = exact_dot(owned0, sel0, (((1,), (1,)), ((), ())))
    update0 = apply_kernel(delta0, kern(points, block_pts0))
    residual = residual - update0 - ridge_weight * spread0
    coef = coef + spread0
    kernel1 = kern(points, block_pts1)

    delta1 = solve(block_res1, block1)
    owned1 = lax.dynamic_slice_in_dim(delta1, mine * per, per, axis=1)
    spread1 = exact_dot(owned1, sel1, (((1,), (1,)), ((), ())))
    update1 = apply_kernel(delta1, kernel1)
    residual = residual - update1 - ridge_weight * spread1
    coef = coef + spread1
    return (residual, coef)


def solution(mesh):
    in_specs = (
        P(None, ("grp", "mem")),
        P(None, ("grp", "mem")),
        P(None, ("grp", "mem")),
        P(("grp", "mem")),
        P(),
        P("grp", "mem", None),
    )
    out_specs = (P(None, ("grp", "mem")), P(None, ("grp", "mem")))
    return jax.shard_map(body, mesh=mesh, in_specs=in_specs, out_specs=out_specs, check_vma=False)
```

```python
import jax
import jax.numpy as jnp
from jax import lax
from jax.sharding import PartitionSpec as P
from jax.experimental import pallas as pl
from jax.experimental.pallas import tpu as pltpu

B = 4096
STEPS = 2

ridge_weight = 0.5
kernel_scale = 0.125
ALL = ("grp", "mem")
HIGHEST = lax.Precision.HIGHEST
HIGH = lax.Precision.HIGH


def gather_all(piece, n_dev):
    sent = jnp.broadcast_to(piece[None], (n_dev,) + piece.shape)
    return lax.all_to_all(sent, ALL, 0, 0, tiled=True)


def split3(x):
    x1 = lax.reduce_precision(x, exponent_bits=8, mantissa_bits=7)
    r1 = x - x1
    x2 = lax.reduce_precision(r1, exponent_bits=8, mantissa_bits=7)
    r2 = r1 - x2
    return x1.astype(jnp.bfloat16), x2.astype(jnp.bfloat16), r2.astype(jnp.bfloat16)


def kern(u, v):
    nu = jnp.sum(u * u, axis=0, keepdims=True)
    nv = jnp.sum(v * v, axis=0, keepdims=True)
    u1, u2, u3 = split3(u)
    v1, v2, v3 = split3(-2.0 * v)
    a1, a2, a3 = split3(nu)
    b1, b2, b3 = split3(nv)
    one_u = jnp.ones_like(a1)
    one_v = jnp.ones_like(b1)
    left = jnp.concatenate([u1, u1, u2, u1, u3, u2, a1, a2, a3, one_u, one_u, one_u], axis=0)
    right = jnp.concatenate([v1, v2, v1, v3, v1, v2, one_v, one_v, one_v, b1, b2, b3], axis=0)
    dist = lax.dot_general(left, right, (((0,), (0,)), ((), ())), preferred_element_type=jnp.float32)
    kernel = jnp.exp(-kernel_scale * dist)
    k1 = lax.reduce_precision(kernel, exponent_bits=8, mantissa_bits=7)
    return k1.astype(jnp.bfloat16), (kernel - k1).astype(jnp.bfloat16)


def apply_kernel(delta, kernel):
    k1, k2 = kernel
    d1f = lax.reduce_precision(delta, exponent_bits=8, mantissa_bits=7)
    d1 = d1f.astype(jnp.bfloat16)
    d2 = (delta - d1f).astype(jnp.bfloat16)
    rows = delta.shape[0]
    dims = (((1,), (1,)), ((), ()))
    both = lax.dot_general(jnp.concatenate([d1, d2], axis=0), k1, dims, preferred_element_type=jnp.float32)
    low = lax.dot_general(d1, k2, dims, preferred_element_type=jnp.float32)
    return (both[:rows] + both[rows:]) + low


def exact_dot(x, onehot, dims):
    rows = x.shape[0]
    parts = jnp.concatenate(split3(x), axis=0)
    out = lax.dot_general(parts, onehot, dims, preferred_element_type=jnp.float32)
    return (out[:rows] + out[rows:2 * rows]) + out[2 * rows:]


def solve_kernel(slot_ref, inv_ref, rcat_ref, r1_ref, o_ref):
    a = inv_ref[...]
    hi = a.astype(jnp.bfloat16)
    lo = (a - hi.astype(jnp.float32)).astype(jnp.bfloat16)
    dims = (((1,), (1,)), ((), ()))
    both = lax.dot_general(rcat_ref[...], hi, dims, preferred_element_type=jnp.float32)
    low = lax.dot_general(r1_ref[...], lo, dims, preferred_element_type=jnp.float32)
    rows = o_ref.shape[0]
    o_ref[...] = (both[:rows] + both[rows:]) + low


def solve_rows(inverse, slot, block_res, tile=256):
    _, n, width = inverse.shape
    rows = block_res.shape[0]
    r1f = lax.reduce_precision(block_res, exponent_bits=8, mantissa_bits=7)
    r1 = r1f.astype(jnp.bfloat16)
    r2 = (block_res - r1f).astype(jnp.bfloat16)
    rcat = jnp.concatenate([r1, r2], axis=0)
    tile = min(tile, n)
    grid_spec = pltpu.PrefetchScalarGridSpec(
        num_scalar_prefetch=1,
        grid=(n // tile,),
        in_specs=[
            pl.BlockSpec((None, tile, width), lambda i, s: (s[0], i, 0)),
            pl.BlockSpec((2 * rows, width), lambda i, s: (0, 0)),
            pl.BlockSpec((rows, width), lambda i, s: (0, 0)),
        ],
        out_specs=pl.BlockSpec((rows, tile), lambda i, s: (0, i)),
    )
    return pl.pallas_call(
        solve_kernel,
        grid_spec=grid_spec,
        out_shape=jax.ShapeDtypeStruct((rows, n), jnp.float32),
        compiler_params=pltpu.CompilerParams(vmem_limit_bytes=48 * 1024 * 1024),
        cost_estimate=pl.CostEstimate(
            flops=6 * rows * n * width, transcendentals=0, bytes_accessed=4 * n * width
        ),
    )(jnp.reshape(slot, (1,)).astype(jnp.int32), inverse, rcat, r1)


def body(points, residual, coef, block_of, order, inverse):
    n_grp = lax.axis_size("grp")
    n_mem = lax.axis_size("mem")
    n_dev = n_grp * n_mem
    per = B // n_dev
    slots = inverse.shape[0]
    feat = points.shape[0]
    rhs = residual.shape[0]
    mine = lax.axis_index("grp") * n_mem + lax.axis_index("mem")

    def selector(block_id):
        inside = block_of == block_id
        position = jnp.cumsum(inside.astype(jnp.int32)) - 1
        return (
            (position[:, None] == jnp.arange(per, dtype=jnp.int32)[None, :]) & inside[:, None]
        ).astype(jnp.bfloat16)

    def solve(block_res, block_id):
        solved = solve_rows(inverse, block_id % slots, block_res)
        owner = block_id // slots
        pieces = jnp.transpose(solved.reshape(rhs, n_grp, per), (1, 0, 2))
        scattered = lax.all_to_all(pieces, "grp", 0, 0, tiled=True)
        piece = lax.dynamic_index_in_dim(scattered, owner, 0, keepdims=False)
        pieces_all = gather_all(piece, n_dev)
        pieces_all = jnp.transpose(pieces_all.reshape(n_grp, n_mem, rhs, per), (2, 1, 0, 3))
        return pieces_all.reshape(rhs, B)

    def to_block(gathered, rows):
        return jnp.transpose(gathered, (1, 0, 2)).reshape(rows, B)

    block0, block1 = order[0], order[1]
    sel0 = selector(block0)
    sel1 = selector(block1)
    plain = (((1,), (0,)), ((), ()))
    chosen = exact_dot(
        jnp.concatenate([residual, points], axis=0), jnp.concatenate([sel0, sel1], axis=1), plain
    )
    chosen0 = chosen[:, :per]
    res1_start = chosen[:rhs, per:]
    pts1_local = chosen[rhs:, per:]
    gathered = to_block(gather_all(jnp.concatenate([chosen0, pts1_local], axis=0), n_dev), rhs + 2 * feat)
    block_res0 = gathered[:rhs]
    block_pts0 = gathered[rhs:rhs + feat]
    block_pts1 = gathered[rhs + feat:]

    delta0 = solve(block_res0, block0)
    owned0 = lax.dynamic_slice_in_dim(delta0, mine * per, per, axis=1)
    early = apply_kernel(delta0, kern(pts1_local, block_pts0))
    overlap = lax.dot_general(sel0, sel1, (((0,), (0,)), ((), ())), preferred_element_type=jnp.float32)
    overlap = overlap.astype(jnp.bfloat16)
    res1_local = res1_start - early - ridge_weight * exact_dot(owned0, overlap, plain)
    block_res1 = to_block(gather_all(res1_local, n_dev), rhs)

    spread0 = exact_dot(owned0, sel0, (((1,), (1,)), ((), ())))
    update0 = apply_kernel(delta0, kern(points, block_pts0))
    residual = residual - update0 - ridge_weight * spread0
    coef = coef + spread0
    kernel1 = kern(points, block_pts1)

    delta1 = solve(block_res1, block1)
    owned1 = lax.dynamic_slice_in_dim(delta1, mine * per, per, axis=1)
    spread1 = exact_dot(owned1, sel1, (((1,), (1,)), ((), ())))
    update1 = apply_kernel(delta1, kernel1)
    residual = residual - update1 - ridge_weight * spread1
    coef = coef + spread1
    return (residual, coef)


def solution(mesh):
    in_specs = (
        P(None, ("grp", "mem")),
        P(None, ("grp", "mem")),
        P(None, ("grp", "mem")),
        P(("grp", "mem")),
        P(),
        P("grp", "mem", None),
    )
    out_specs = (P(None, ("grp", "mem")), P(None, ("grp", "mem")))
    return jax.shard_map(body, mesh=mesh, in_specs=in_specs, out_specs=out_specs, check_vma=False)
```

```python
import jax
import jax.numpy as jnp
from jax import lax
from jax.sharding import PartitionSpec as P
from jax.experimental import pallas as pl
from jax.experimental.pallas import tpu as pltpu

B = 4096
STEPS = 2

ridge_weight = 0.5
kernel_scale = 0.125
ALL = ("grp", "mem")
HIGHEST = lax.Precision.HIGHEST
HIGH = lax.Precision.HIGH


def gather_all(piece, n_dev):
    sent = jnp.broadcast_to(piece[None], (n_dev,) + piece.shape)
    return lax.all_to_all(sent, ALL, 0, 0, tiled=True)


def split3(x):
    x1 = lax.reduce_precision(x, exponent_bits=8, mantissa_bits=7)
    r1 = x - x1
    x2 = lax.reduce_precision(r1, exponent_bits=8, mantissa_bits=7)
    r2 = r1 - x2
    return x1.astype(jnp.bfloat16), x2.astype(jnp.bfloat16), r2.astype(jnp.bfloat16)


def update_kernel(left_ref, right_ref, d12_ref, d1_ref, o_ref, acc1, acc2):
    j = pl.program_id(1)

    @pl.when(j == 0)
    def _():
        acc1[...] = jnp.zeros_like(acc1)
        acc2[...] = jnp.zeros_like(acc2)

    dist = jnp.dot(left_ref[...], right_ref[...], preferred_element_type=jnp.float32)
    kernel = jnp.exp(-kernel_scale * dist)
    k1 = kernel.astype(jnp.bfloat16)
    k2 = (kernel - k1.astype(jnp.float32)).astype(jnp.bfloat16)
    acc1[...] += jnp.dot(k1, d12_ref[...], preferred_element_type=jnp.float32)
    acc2[...] += jnp.dot(k2, d1_ref[...], preferred_element_type=jnp.float32)

    @pl.when(j == pl.num_programs(1) - 1)
    def _():
        rows = o_ref.shape[1]
        o_ref[...] = (acc1[:, :rows] + acc1[:, rows:]) + acc2[...]


def kernel_update(u, v, delta, tile_n=256, tile_m=512):
    n = u.shape[1]
    m = v.shape[1]
    rows = delta.shape[0]
    nu = jnp.sum(u * u, axis=0, keepdims=True)
    nv = jnp.sum(v * v, axis=0, keepdims=True)
    u1, u2, u3 = split3(u)
    v1, v2, v3 = split3(-2.0 * v)
    a1, a2, a3 = split3(nu)
    b1, b2, b3 = split3(nv)
    one_u = jnp.ones_like(a1)
    one_v = jnp.ones_like(b1)
    left = jnp.concatenate([u1, u1, u2, u1, u3, u2, a1, a2, a3, one_u, one_u, one_u], axis=0)
    right = jnp.concatenate([v1, v2, v1, v3, v1, v2, one_v, one_v, one_v, b1, b2, b3], axis=0)
    depth = 128
    left = jnp.pad(left, ((0, depth - left.shape[0]), (0, 0))).T
    right = jnp.pad(right, ((0, depth - right.shape[0]), (0, 0)))
    d1f = lax.reduce_precision(delta, exponent_bits=8, mantissa_bits=7)
    d1 = d1f.astype(jnp.bfloat16)
    d2 = (delta - d1f).astype(jnp.bfloat16)
    d12 = jnp.concatenate([d1, d2], axis=0).T
    d1t = d1.T
    tile_n = min(tile_n, n)
    tile_m = min(tile_m, m)
    out = pl.pallas_call(
        update_kernel,
        grid=(n // tile_n, m // tile_m),
        in_specs=[
            pl.BlockSpec((tile_n, depth), lambda i, j: (i, 0)),
            pl.BlockSpec((depth, tile_m), lambda i, j: (0, j)),
            pl.BlockSpec((tile_m, 2 * rows), lambda i, j: (j, 0)),
            pl.BlockSpec((tile_m, rows), lambda i, j: (j, 0)),
        ],
        out_specs=pl.BlockSpec((tile_n, rows), lambda i, j: (i, 0)),
        out_shape=jax.ShapeDtypeStruct((n, rows), jnp.float32),
        scratch_shapes=[
            pltpu.VMEM((tile_n, 2 * rows), jnp.float32),
            pltpu.VMEM((tile_n, rows), jnp.float32),
        ],
        cost_estimate=pl.CostEstimate(
            flops=2 * n * m * (depth + 3 * rows), transcendentals=n * m,
            bytes_accessed=2 * (n + m) * depth + 6 * m * rows + 4 * n * rows,
        ),
    )(left, right, d12, d1t)
    return out.T


def exact_dot(x, onehot, dims):
    rows = x.shape[0]
    parts = jnp.concatenate(split3(x), axis=0)
    out = lax.dot_general(parts, onehot, dims, preferred_element_type=jnp.float32)
    return (out[:rows] + out[rows:2 * rows]) + out[2 * rows:]


def solve_kernel(slot_ref, inv_ref, rcat_ref, r1_ref, o_ref):
    a = inv_ref[...]
    hi = a.astype(jnp.bfloat16)
    lo = (a - hi.astype(jnp.float32)).astype(jnp.bfloat16)
    dims = (((1,), (1,)), ((), ()))
    both = lax.dot_general(rcat_ref[...], hi, dims, preferred_element_type=jnp.float32)
    low = lax.dot_general(r1_ref[...], lo, dims, preferred_element_type=jnp.float32)
    rows = o_ref.shape[0]
    o_ref[...] = (both[:rows] + both[rows:]) + low


def solve_rows(inverse, slot, block_res, tile=256):
    _, n, width = inverse.shape
    rows = block_res.shape[0]
    r1f = lax.reduce_precision(block_res, exponent_bits=8, mantissa_bits=7)
    r1 = r1f.astype(jnp.bfloat16)
    r2 = (block_res - r1f).astype(jnp.bfloat16)
    rcat = jnp.concatenate([r1, r2], axis=0)
    tile = min(tile, n)
    grid_spec = pltpu.PrefetchScalarGridSpec(
        num_scalar_prefetch=1,
        grid=(n // tile,),
        in_specs=[
            pl.BlockSpec((None, tile, width), lambda i, s: (s[0], i, 0)),
            pl.BlockSpec((2 * rows, width), lambda i, s: (0, 0)),
            pl.BlockSpec((rows, width), lambda i, s: (0, 0)),
        ],
        out_specs=pl.BlockSpec((rows, tile), lambda i, s: (0, i)),
    )
    return pl.pallas_call(
        solve_kernel,
        grid_spec=grid_spec,
        out_shape=jax.ShapeDtypeStruct((rows, n), jnp.float32),
        compiler_params=pltpu.CompilerParams(vmem_limit_bytes=48 * 1024 * 1024),
        cost_estimate=pl.CostEstimate(
            flops=6 * rows * n * width, transcendentals=0, bytes_accessed=4 * n * width
        ),
    )(jnp.reshape(slot, (1,)).astype(jnp.int32), inverse, rcat, r1)


def body(points, residual, coef, block_of, order, inverse):
    n_grp = lax.axis_size("grp")
    n_mem = lax.axis_size("mem")
    n_dev = n_grp * n_mem
    per = B // n_dev
    slots = inverse.shape[0]
    feat = points.shape[0]
    rhs = residual.shape[0]
    mine = lax.axis_index("grp") * n_mem + lax.axis_index("mem")

    def selector(block_id):
        inside = block_of == block_id
        position = jnp.cumsum(inside.astype(jnp.int32)) - 1
        return (
            (position[:, None] == jnp.arange(per, dtype=jnp.int32)[None, :]) & inside[:, None]
        ).astype(jnp.bfloat16)

    def solve(block_res, block_id):
        solved = solve_rows(inverse, block_id % slots, block_res)
        owner = block_id // slots
        pieces = jnp.transpose(solved.reshape(rhs, n_grp, per), (1, 0, 2))
        scattered = lax.all_to_all(pieces, "grp", 0, 0, tiled=True)
        piece = lax.dynamic_index_in_dim(scattered, owner, 0, keepdims=False)
        pieces_all = gather_all(piece, n_dev)
        pieces_all = jnp.transpose(pieces_all.reshape(n_grp, n_mem, rhs, per), (2, 1, 0, 3))
        return pieces_all.reshape(rhs, B)

    def to_block(gathered, rows):
        return jnp.transpose(gathered, (1, 0, 2)).reshape(rows, B)

    block0, block1 = order[0], order[1]
    sel0 = selector(block0)
    sel1 = selector(block1)
    plain = (((1,), (0,)), ((), ()))
    chosen = exact_dot(
        jnp.concatenate([residual, points], axis=0), jnp.concatenate([sel0, sel1], axis=1), plain
    )
    chosen0 = chosen[:, :per]
    res1_start = chosen[:rhs, per:]
    pts1_local = chosen[rhs:, per:]
    gathered = to_block(gather_all(jnp.concatenate([chosen0, pts1_local], axis=0), n_dev), rhs + 2 * feat)
    block_res0 = gathered[:rhs]
    block_pts0 = gathered[rhs:rhs + feat]
    block_pts1 = gathered[rhs + feat:]

    delta0 = solve(block_res0, block0)
    owned0 = lax.dynamic_slice_in_dim(delta0, mine * per, per, axis=1)
    early = kernel_update(pts1_local, block_pts0, delta0)
    overlap = lax.dot_general(sel0, sel1, (((0,), (0,)), ((), ())), preferred_element_type=jnp.float32)
    overlap = overlap.astype(jnp.bfloat16)
    res1_local = res1_start - early - ridge_weight * exact_dot(owned0, overlap, plain)
    block_res1 = to_block(gather_all(res1_local, n_dev), rhs)

    spread0 = exact_dot(owned0, sel0, (((1,), (1,)), ((), ())))
    update0 = kernel_update(points, block_pts0, delta0)
    residual = residual - update0 - ridge_weight * spread0
    coef = coef + spread0

    delta1 = solve(block_res1, block1)
    owned1 = lax.dynamic_slice_in_dim(delta1, mine * per, per, axis=1)
    spread1 = exact_dot(owned1, sel1, (((1,), (1,)), ((), ())))
    update1 = kernel_update(points, block_pts1, delta1)
    residual = residual - update1 - ridge_weight * spread1
    coef = coef + spread1
    return (residual, coef)


def solution(mesh):
    in_specs = (
        P(None, ("grp", "mem")),
        P(None, ("grp", "mem")),
        P(None, ("grp", "mem")),
        P(("grp", "mem")),
        P(),
        P("grp", "mem", None),
    )
    out_specs = (P(None, ("grp", "mem")), P(None, ("grp", "mem")))
    return jax.shard_map(body, mesh=mesh, in_specs=in_specs, out_specs=out_specs, check_vma=False)
```

```python
import jax
import jax.numpy as jnp
from jax import lax
from jax.sharding import PartitionSpec as P
from jax.experimental import pallas as pl
from jax.experimental.pallas import tpu as pltpu

B = 4096
STEPS = 2

ridge_weight = 0.5
kernel_scale = 0.125
ALL = ("grp", "mem")
HIGHEST = lax.Precision.HIGHEST
HIGH = lax.Precision.HIGH


def gather_all(piece, n_dev):
    sent = jnp.broadcast_to(piece[None], (n_dev,) + piece.shape)
    return lax.all_to_all(sent, ALL, 0, 0, tiled=True)


def split3(x):
    x1 = lax.reduce_precision(x, exponent_bits=8, mantissa_bits=7)
    r1 = x - x1
    x2 = lax.reduce_precision(r1, exponent_bits=8, mantissa_bits=7)
    r2 = r1 - x2
    return x1.astype(jnp.bfloat16), x2.astype(jnp.bfloat16), r2.astype(jnp.bfloat16)


def kern(u, v):
    nu = jnp.sum(u * u, axis=0, keepdims=True)
    nv = jnp.sum(v * v, axis=0, keepdims=True)
    u1, u2, u3 = split3(u)
    v1, v2, v3 = split3(-2.0 * v)
    a1, a2, a3 = split3(nu)
    b1, b2, b3 = split3(nv)
    one_u = jnp.ones_like(a1)
    one_v = jnp.ones_like(b1)
    left = jnp.concatenate([u1, u1, u2, u1, u3, u2, a1, a2, a3, one_u, one_u, one_u], axis=0)
    right = jnp.concatenate([v1, v2, v1, v3, v1, v2, one_v, one_v, one_v, b1, b2, b3], axis=0)
    dist = lax.dot_general(left, right, (((0,), (0,)), ((), ())), preferred_element_type=jnp.float32)
    kernel = jnp.exp(-kernel_scale * dist)
    k1 = lax.reduce_precision(kernel, exponent_bits=8, mantissa_bits=7)
    return lax.optimization_barrier((k1.astype(jnp.bfloat16), (kernel - k1).astype(jnp.bfloat16)))


def apply_kernel(delta, kernel):
    k1, k2 = kernel
    d1f = lax.reduce_precision(delta, exponent_bits=8, mantissa_bits=7)
    d1 = d1f.astype(jnp.bfloat16)
    d2 = (delta - d1f).astype(jnp.bfloat16)
    rows = delta.shape[0]
    dims = (((1,), (1,)), ((), ()))
    both = lax.dot_general(jnp.concatenate([d1, d2], axis=0), k1, dims, preferred_element_type=jnp.float32)
    low = lax.dot_general(d1, k2, dims, preferred_element_type=jnp.float32)
    return (both[:rows] + both[rows:]) + low


def exact_dot(x, onehot, dims):
    rows = x.shape[0]
    parts = jnp.concatenate(split3(x), axis=0)
    out = lax.dot_general(parts, onehot, dims, preferred_element_type=jnp.float32)
    return (out[:rows] + out[rows:2 * rows]) + out[2 * rows:]


def solve_kernel(slot_ref, inv_ref, rcat_ref, r1_ref, o_ref):
    a = inv_ref[...]
    hi = a.astype(jnp.bfloat16)
    lo = (a - hi.astype(jnp.float32)).astype(jnp.bfloat16)
    dims = (((1,), (1,)), ((), ()))
    both = lax.dot_general(rcat_ref[...], hi, dims, preferred_element_type=jnp.float32)
    low = lax.dot_general(r1_ref[...], lo, dims, preferred_element_type=jnp.float32)
    rows = o_ref.shape[0]
    o_ref[...] = (both[:rows] + both[rows:]) + low


def solve_rows(inverse, slot, block_res, tile=256):
    _, n, width = inverse.shape
    rows = block_res.shape[0]
    r1f = lax.reduce_precision(block_res, exponent_bits=8, mantissa_bits=7)
    r1 = r1f.astype(jnp.bfloat16)
    r2 = (block_res - r1f).astype(jnp.bfloat16)
    rcat = jnp.concatenate([r1, r2], axis=0)
    tile = min(tile, n)
    grid_spec = pltpu.PrefetchScalarGridSpec(
        num_scalar_prefetch=1,
        grid=(n // tile,),
        in_specs=[
            pl.BlockSpec((None, tile, width), lambda i, s: (s[0], i, 0)),
            pl.BlockSpec((2 * rows, width), lambda i, s: (0, 0)),
            pl.BlockSpec((rows, width), lambda i, s: (0, 0)),
        ],
        out_specs=pl.BlockSpec((rows, tile), lambda i, s: (0, i)),
    )
    return pl.pallas_call(
        solve_kernel,
        grid_spec=grid_spec,
        out_shape=jax.ShapeDtypeStruct((rows, n), jnp.float32),
        compiler_params=pltpu.CompilerParams(vmem_limit_bytes=48 * 1024 * 1024),
        cost_estimate=pl.CostEstimate(
            flops=6 * rows * n * width, transcendentals=0, bytes_accessed=4 * n * width
        ),
    )(jnp.reshape(slot, (1,)).astype(jnp.int32), inverse, rcat, r1)


def body(points, residual, coef, block_of, order, inverse):
    n_grp = lax.axis_size("grp")
    n_mem = lax.axis_size("mem")
    n_dev = n_grp * n_mem
    per = B // n_dev
    slots = inverse.shape[0]
    feat = points.shape[0]
    rhs = residual.shape[0]
    mine = lax.axis_index("grp") * n_mem + lax.axis_index("mem")

    def selector(block_id):
        inside = block_of == block_id
        position = jnp.cumsum(inside.astype(jnp.int32)) - 1
        return (
            (position[:, None] == jnp.arange(per, dtype=jnp.int32)[None, :]) & inside[:, None]
        ).astype(jnp.bfloat16)

    def solve(block_res, block_id):
        solved = solve_rows(inverse, block_id % slots, block_res)
        owner = block_id // slots
        pieces = jnp.transpose(solved.reshape(rhs, n_grp, per), (1, 0, 2))
        scattered = lax.all_to_all(pieces, "grp", 0, 0, tiled=True)
        piece = lax.dynamic_index_in_dim(scattered, owner, 0, keepdims=False)
        pieces_all = gather_all(piece, n_dev)
        pieces_all = jnp.transpose(pieces_all.reshape(n_grp, n_mem, rhs, per), (2, 1, 0, 3))
        return pieces_all.reshape(rhs, B)

    def to_block(gathered, rows):
        return jnp.transpose(gathered, (1, 0, 2)).reshape(rows, B)

    block0, block1 = order[0], order[1]
    sel0 = selector(block0)
    sel1 = selector(block1)
    plain = (((1,), (0,)), ((), ()))
    chosen = exact_dot(
        jnp.concatenate([residual, points], axis=0), jnp.concatenate([sel0, sel1], axis=1), plain
    )
    chosen0 = chosen[:, :per]
    res1_start = chosen[:rhs, per:]
    pts1_local = chosen[rhs:, per:]
    gathered = to_block(gather_all(jnp.concatenate([chosen0, pts1_local], axis=0), n_dev), rhs + 2 * feat)
    block_res0 = gathered[:rhs]
    block_pts0 = gathered[rhs:rhs + feat]
    block_pts1 = gathered[rhs + feat:]

    delta0 = solve(block_res0, block0)
    owned0 = lax.dynamic_slice_in_dim(delta0, mine * per, per, axis=1)
    early = apply_kernel(delta0, kern(pts1_local, block_pts0))
    overlap = lax.dot_general(sel0, sel1, (((0,), (0,)), ((), ())), preferred_element_type=jnp.float32)
    overlap = overlap.astype(jnp.bfloat16)
    res1_local = res1_start - early - ridge_weight * exact_dot(owned0, overlap, plain)
    block_res1 = to_block(gather_all(res1_local, n_dev), rhs)

    spread0 = exact_dot(owned0, sel0, (((1,), (1,)), ((), ())))
    update0 = apply_kernel(delta0, kern(points, block_pts0))
    residual = residual - update0 - ridge_weight * spread0
    coef = coef + spread0
    kernel1 = kern(points, block_pts1)

    delta1 = solve(block_res1, block1)
    owned1 = lax.dynamic_slice_in_dim(delta1, mine * per, per, axis=1)
    spread1 = exact_dot(owned1, sel1, (((1,), (1,)), ((), ())))
    update1 = apply_kernel(delta1, kernel1)
    residual = residual - update1 - ridge_weight * spread1
    coef = coef + spread1
    return (residual, coef)


def solution(mesh):
    in_specs = (
        P(None, ("grp", "mem")),
        P(None, ("grp", "mem")),
        P(None, ("grp", "mem")),
        P(("grp", "mem")),
        P(),
        P("grp", "mem", None),
    )
    out_specs = (P(None, ("grp", "mem")), P(None, ("grp", "mem")))
    return jax.shard_map(body, mesh=mesh, in_specs=in_specs, out_specs=out_specs, check_vma=False)
```

```python
import jax
import jax.numpy as jnp
from jax import lax
from jax.sharding import PartitionSpec as P
from jax.experimental import pallas as pl
from jax.experimental.pallas import tpu as pltpu

B = 4096
STEPS = 2

ridge_weight = 0.5
kernel_scale = 0.125
ALL = ("grp", "mem")
HIGHEST = lax.Precision.HIGHEST
HIGH = lax.Precision.HIGH


def gather_all(piece, n_dev):
    sent = jnp.broadcast_to(piece[None], (n_dev,) + piece.shape)
    return lax.all_to_all(sent, ALL, 0, 0, tiled=True)


def split3(x):
    x1 = lax.reduce_precision(x, exponent_bits=8, mantissa_bits=7)
    r1 = x - x1
    x2 = lax.reduce_precision(r1, exponent_bits=8, mantissa_bits=7)
    r2 = r1 - x2
    return x1.astype(jnp.bfloat16), x2.astype(jnp.bfloat16), r2.astype(jnp.bfloat16)


def kern(u, v):
    nu = jnp.sum(u * u, axis=0, keepdims=True)
    nv = jnp.sum(v * v, axis=0, keepdims=True)
    u1, u2, u3 = split3(u)
    v1, v2, v3 = split3(-2.0 * v)
    a1, a2, a3 = split3(nu)
    b1, b2, b3 = split3(nv)
    one_u = jnp.ones_like(a1)
    one_v = jnp.ones_like(b1)
    left = jnp.concatenate([u1, u1, u2, u1, u3, u2, a1, a2, a3, one_u, one_u, one_u], axis=0)
    right = jnp.concatenate([v1, v2, v1, v3, v1, v2, one_v, one_v, one_v, b1, b2, b3], axis=0)
    dist = lax.dot_general(left, right, (((0,), (0,)), ((), ())), preferred_element_type=jnp.float32)
    kernel = jnp.exp(-kernel_scale * dist)
    k1 = lax.reduce_precision(kernel, exponent_bits=8, mantissa_bits=7)
    return lax.optimization_barrier((k1.astype(jnp.bfloat16), (kernel - k1).astype(jnp.bfloat16)))


def apply_kernel(delta, kernel):
    k1, k2 = kernel
    d1f = lax.reduce_precision(delta, exponent_bits=8, mantissa_bits=7)
    d1 = d1f.astype(jnp.bfloat16)
    d2 = (delta - d1f).astype(jnp.bfloat16)
    rows = delta.shape[0]
    dims = (((1,), (1,)), ((), ()))
    both = lax.dot_general(jnp.concatenate([d1, d2], axis=0), k1, dims, preferred_element_type=jnp.float32)
    low = lax.dot_general(d1, k2, dims, preferred_element_type=jnp.float32)
    return (both[:rows] + both[rows:]) + low


def exact_dot(x, onehot, dims):
    rows = x.shape[0]
    parts = jnp.concatenate(split3(x), axis=0)
    out = lax.dot_general(parts, onehot, dims, preferred_element_type=jnp.float32)
    return (out[:rows] + out[rows:2 * rows]) + out[2 * rows:]


def solve_kernel(slot_ref, inv_ref, rcat_ref, r1_ref, o_ref):
    a = inv_ref[...]
    hi = a.astype(jnp.bfloat16)
    lo = (a - hi.astype(jnp.float32)).astype(jnp.bfloat16)
    dims = (((1,), (1,)), ((), ()))
    both = lax.dot_general(rcat_ref[...], hi, dims, preferred_element_type=jnp.float32)
    low = lax.dot_general(r1_ref[...], lo, dims, preferred_element_type=jnp.float32)
    rows = o_ref.shape[0]
    o_ref[...] = (both[:rows] + both[rows:]) + low


def solve_rows(inverse, slot, block_res, tile=256):
    _, n, width = inverse.shape
    rows = block_res.shape[0]
    r1f = lax.reduce_precision(block_res, exponent_bits=8, mantissa_bits=7)
    r1 = r1f.astype(jnp.bfloat16)
    r2 = (block_res - r1f).astype(jnp.bfloat16)
    rcat = jnp.concatenate([r1, r2], axis=0)
    tile = min(tile, n)
    grid_spec = pltpu.PrefetchScalarGridSpec(
        num_scalar_prefetch=1,
        grid=(n // tile,),
        in_specs=[
            pl.BlockSpec((None, tile, width), lambda i, s: (s[0], i, 0)),
            pl.BlockSpec((2 * rows, width), lambda i, s: (0, 0)),
            pl.BlockSpec((rows, width), lambda i, s: (0, 0)),
        ],
        out_specs=pl.BlockSpec((rows, tile), lambda i, s: (0, i)),
    )
    return pl.pallas_call(
        solve_kernel,
        grid_spec=grid_spec,
        out_shape=jax.ShapeDtypeStruct((rows, n), jnp.float32),
        compiler_params=pltpu.CompilerParams(vmem_limit_bytes=48 * 1024 * 1024),
        cost_estimate=pl.CostEstimate(
            flops=6 * rows * n * width, transcendentals=0, bytes_accessed=4 * n * width
        ),
    )(jnp.reshape(slot, (1,)).astype(jnp.int32), inverse, rcat, r1)


def body(points, residual, coef, block_of, order, inverse):
    n_grp = lax.axis_size("grp")
    n_mem = lax.axis_size("mem")
    n_dev = n_grp * n_mem
    per = B // n_dev
    slots = inverse.shape[0]
    feat = points.shape[0]
    rhs = residual.shape[0]
    mine = lax.axis_index("grp") * n_mem + lax.axis_index("mem")

    def selector(block_id):
        inside = block_of == block_id
        position = jnp.cumsum(inside.astype(jnp.int32)) - 1
        return (
            (position[:, None] == jnp.arange(per, dtype=jnp.int32)[None, :]) & inside[:, None]
        ).astype(jnp.bfloat16)

    def solve(block_res, block_id):
        solved = solve_rows(inverse, block_id % slots, block_res)
        owner = block_id // slots
        pieces = jnp.transpose(solved.reshape(rhs, n_grp, per), (1, 0, 2))
        scattered = lax.all_to_all(pieces, "grp", 0, 0, tiled=True)
        piece = lax.dynamic_index_in_dim(scattered, owner, 0, keepdims=False)
        pieces_all = gather_all(piece, n_dev)
        pieces_all = jnp.transpose(pieces_all.reshape(n_grp, n_mem, rhs, per), (2, 1, 0, 3))
        return pieces_all.reshape(rhs, B)

    def to_block(gathered, rows):
        return jnp.transpose(gathered, (1, 0, 2)).reshape(rows, B)

    block0, block1 = order[0], order[1]
    sel0 = selector(block0)
    sel1 = selector(block1)
    plain = (((1,), (0,)), ((), ()))
    chosen = exact_dot(
        jnp.concatenate([residual, points], axis=0), jnp.concatenate([sel0, sel1], axis=1), plain
    )
    chosen0 = chosen[:, :per]
    res1_start = chosen[:rhs, per:]
    pts1_local = chosen[rhs:, per:]
    gathered = to_block(gather_all(jnp.concatenate([chosen0, pts1_local], axis=0), n_dev), rhs + 2 * feat)
    block_res0 = gathered[:rhs]
    block_pts0 = gathered[rhs:rhs + feat]
    block_pts1 = gathered[rhs + feat:]

    delta0 = solve(block_res0, block0)
    owned0 = lax.dynamic_slice_in_dim(delta0, mine * per, per, axis=1)
    early = apply_kernel(delta0, kern(pts1_local, block_pts0))
    overlap = lax.dot_general(sel0, sel1, (((0,), (0,)), ((), ())), preferred_element_type=jnp.float32)
    overlap = overlap.astype(jnp.bfloat16)
    res1_local = res1_start - early - ridge_weight * exact_dot(owned0, overlap, plain)
    res1_local, pts_late, pts0_late, pts1_late = lax.optimization_barrier(
        (res1_local, points, block_pts0, block_pts1)
    )
    block_res1 = to_block(gather_all(res1_local, n_dev), rhs)

    spread0 = exact_dot(owned0, sel0, (((1,), (1,)), ((), ())))
    update0 = apply_kernel(delta0, kern(pts_late, pts0_late))
    residual = residual - update0 - ridge_weight * spread0
    coef = coef + spread0
    kernel1 = kern(pts_late, pts1_late)

    delta1 = solve(block_res1, block1)
    owned1 = lax.dynamic_slice_in_dim(delta1, mine * per, per, axis=1)
    spread1 = exact_dot(owned1, sel1, (((1,), (1,)), ((), ())))
    update1 = apply_kernel(delta1, kernel1)
    residual = residual - update1 - ridge_weight * spread1
    coef = coef + spread1
    return (residual, coef)


def solution(mesh):
    in_specs = (
        P(None, ("grp", "mem")),
        P(None, ("grp", "mem")),
        P(None, ("grp", "mem")),
        P(("grp", "mem")),
        P(),
        P("grp", "mem", None),
    )
    out_specs = (P(None, ("grp", "mem")), P(None, ("grp", "mem")))
    return jax.shard_map(body, mesh=mesh, in_specs=in_specs, out_specs=out_specs, check_vma=False)
```

```python
import jax
import jax.numpy as jnp
from jax import lax
from jax.sharding import PartitionSpec as P
from jax.experimental import pallas as pl
from jax.experimental.pallas import tpu as pltpu

B = 4096
STEPS = 2

ridge_weight = 0.5
kernel_scale = 0.125
ALL = ("grp", "mem")
HIGHEST = lax.Precision.HIGHEST
HIGH = lax.Precision.HIGH


def gather_all(piece, n_dev):
    sent = jnp.broadcast_to(piece[None], (n_dev,) + piece.shape)
    return lax.all_to_all(sent, ALL, 0, 0, tiled=True)


def split3(x):
    x1 = lax.reduce_precision(x, exponent_bits=8, mantissa_bits=7)
    r1 = x - x1
    x2 = lax.reduce_precision(r1, exponent_bits=8, mantissa_bits=7)
    r2 = r1 - x2
    return x1.astype(jnp.bfloat16), x2.astype(jnp.bfloat16), r2.astype(jnp.bfloat16)


def kern(u, v):
    nu = jnp.sum(u * u, axis=0, keepdims=True)
    nv = jnp.sum(v * v, axis=0, keepdims=True)
    u1, u2, u3 = split3(u)
    v1, v2, v3 = split3(-2.0 * v)
    a1, a2, a3 = split3(nu)
    b1, b2, b3 = split3(nv)
    one_u = jnp.ones_like(a1)
    one_v = jnp.ones_like(b1)
    left = jnp.concatenate([u1, u1, u2, u1, u3, u2, a1, a2, a3, one_u, one_u, one_u], axis=0)
    right = jnp.concatenate([v1, v2, v1, v3, v1, v2, one_v, one_v, one_v, b1, b2, b3], axis=0)
    dist = lax.dot_general(left, right, (((0,), (0,)), ((), ())), preferred_element_type=jnp.float32)
    kernel = jnp.exp(-kernel_scale * dist)
    k1 = lax.reduce_precision(kernel, exponent_bits=8, mantissa_bits=7)
    return lax.optimization_barrier((k1.astype(jnp.bfloat16), (kernel - k1).astype(jnp.bfloat16)))


def apply_kernel(delta, kernel):
    k1, k2 = kernel
    d1f = lax.reduce_precision(delta, exponent_bits=8, mantissa_bits=7)
    d1 = d1f.astype(jnp.bfloat16)
    d2 = (delta - d1f).astype(jnp.bfloat16)
    rows = delta.shape[0]
    dims = (((1,), (1,)), ((), ()))
    both = lax.dot_general(jnp.concatenate([d1, d2], axis=0), k1, dims, preferred_element_type=jnp.float32)
    low = lax.dot_general(d1, k2, dims, preferred_element_type=jnp.float32)
    return (both[:rows] + both[rows:]) + low


def exact_dot(x, onehot, dims):
    rows = x.shape[0]
    parts = jnp.concatenate(split3(x), axis=0)
    out = lax.dot_general(parts, onehot, dims, preferred_element_type=jnp.float32)
    return (out[:rows] + out[rows:2 * rows]) + out[2 * rows:]


def solve_kernel(slot_ref, inv_ref, rcat_ref, r1_ref, o_ref):
    a = inv_ref[...]
    hi = a.astype(jnp.bfloat16)
    lo = (a - hi.astype(jnp.float32)).astype(jnp.bfloat16)
    dims = (((1,), (1,)), ((), ()))
    both = lax.dot_general(rcat_ref[...], hi, dims, preferred_element_type=jnp.float32)
    low = lax.dot_general(r1_ref[...], lo, dims, preferred_element_type=jnp.float32)
    rows = o_ref.shape[0]
    o_ref[...] = (both[:rows] + both[rows:]) + low


def solve_rows(inverse, slot, block_res, tile=256):
    _, n, width = inverse.shape
    rows = block_res.shape[0]
    r1f = lax.reduce_precision(block_res, exponent_bits=8, mantissa_bits=7)
    r1 = r1f.astype(jnp.bfloat16)
    r2 = (block_res - r1f).astype(jnp.bfloat16)
    rcat = jnp.concatenate([r1, r2], axis=0)
    tile = min(tile, n)
    grid_spec = pltpu.PrefetchScalarGridSpec(
        num_scalar_prefetch=1,
        grid=(n // tile,),
        in_specs=[
            pl.BlockSpec((None, tile, width), lambda i, s: (s[0], i, 0)),
            pl.BlockSpec((2 * rows, width), lambda i, s: (0, 0)),
            pl.BlockSpec((rows, width), lambda i, s: (0, 0)),
        ],
        out_specs=pl.BlockSpec((rows, tile), lambda i, s: (0, i)),
    )
    return pl.pallas_call(
        solve_kernel,
        grid_spec=grid_spec,
        out_shape=jax.ShapeDtypeStruct((rows, n), jnp.float32),
        compiler_params=pltpu.CompilerParams(vmem_limit_bytes=48 * 1024 * 1024),
        cost_estimate=pl.CostEstimate(
            flops=6 * rows * n * width, transcendentals=0, bytes_accessed=4 * n * width
        ),
    )(jnp.reshape(slot, (1,)).astype(jnp.int32), inverse, rcat, r1)


def body(points, residual, coef, block_of, order, inverse):
    n_grp = lax.axis_size("grp")
    n_mem = lax.axis_size("mem")
    n_dev = n_grp * n_mem
    per = B // n_dev
    slots = inverse.shape[0]
    feat = points.shape[0]
    rhs = residual.shape[0]
    mine = lax.axis_index("grp") * n_mem + lax.axis_index("mem")

    def selector(block_id):
        inside = block_of == block_id
        position = jnp.cumsum(inside.astype(jnp.int32)) - 1
        return (
            (position[:, None] == jnp.arange(per, dtype=jnp.int32)[None, :]) & inside[:, None]
        ).astype(jnp.bfloat16)

    def solve(block_res, block_id):
        return distribute(solve_rows(inverse, block_id % slots, block_res), block_id)

    def distribute(solved, block_id):
        owner = block_id // slots
        pieces = jnp.transpose(solved.reshape(rhs, n_grp, per), (1, 0, 2))
        scattered = lax.all_to_all(pieces, "grp", 0, 0, tiled=True)
        piece = lax.dynamic_index_in_dim(scattered, owner, 0, keepdims=False)
        pieces_all = gather_all(piece, n_dev)
        pieces_all = jnp.transpose(pieces_all.reshape(n_grp, n_mem, rhs, per), (2, 1, 0, 3))
        return pieces_all.reshape(rhs, B)

    def to_block(gathered, rows):
        return jnp.transpose(gathered, (1, 0, 2)).reshape(rows, B)

    block0, block1 = order[0], order[1]
    sel0 = selector(block0)
    sel1 = selector(block1)
    plain = (((1,), (0,)), ((), ()))
    chosen = exact_dot(
        jnp.concatenate([residual, points], axis=0), jnp.concatenate([sel0, sel1], axis=1), plain
    )
    chosen0 = chosen[:, :per]
    res1_start = chosen[:rhs, per:]
    pts1_local = chosen[rhs:, per:]
    gathered = to_block(gather_all(jnp.concatenate([chosen0, pts1_local], axis=0), n_dev), rhs + 2 * feat)
    block_res0 = gathered[:rhs]
    block_pts0 = gathered[rhs:rhs + feat]
    block_pts1 = gathered[rhs + feat:]

    delta0 = solve(block_res0, block0)
    owned0 = lax.dynamic_slice_in_dim(delta0, mine * per, per, axis=1)
    early = apply_kernel(delta0, kern(pts1_local, block_pts0))
    overlap = lax.dot_general(sel0, sel1, (((0,), (0,)), ((), ())), preferred_element_type=jnp.float32)
    overlap = overlap.astype(jnp.bfloat16)
    res1_local = res1_start - early - ridge_weight * exact_dot(owned0, overlap, plain)
    res1_local, pts_late, pts1_late = lax.optimization_barrier((res1_local, points, block_pts1))
    block_res1 = to_block(gather_all(res1_local, n_dev), rhs)
    kernel1 = kern(pts_late, pts1_late)

    solved1 = solve_rows(inverse, block1 % slots, block_res1)
    solved1, pts_later, pts0_later = lax.optimization_barrier((solved1, points, block_pts0))
    delta1 = distribute(solved1, block1)
    spread0 = exact_dot(owned0, sel0, (((1,), (1,)), ((), ())))
    update0 = apply_kernel(delta0, kern(pts_later, pts0_later))
    residual = residual - update0 - ridge_weight * spread0
    coef = coef + spread0

    owned1 = lax.dynamic_slice_in_dim(delta1, mine * per, per, axis=1)
    spread1 = exact_dot(owned1, sel1, (((1,), (1,)), ((), ())))
    update1 = apply_kernel(delta1, kernel1)
    residual = residual - update1 - ridge_weight * spread1
    coef = coef + spread1
    return (residual, coef)


def solution(mesh):
    in_specs = (
        P(None, ("grp", "mem")),
        P(None, ("grp", "mem")),
        P(None, ("grp", "mem")),
        P(("grp", "mem")),
        P(),
        P("grp", "mem", None),
    )
    out_specs = (P(None, ("grp", "mem")), P(None, ("grp", "mem")))
    return jax.shard_map(body, mesh=mesh, in_specs=in_specs, out_specs=out_specs, check_vma=False)
```

```python
import jax
import jax.numpy as jnp
from jax import lax
from jax.sharding import PartitionSpec as P
from jax.experimental import pallas as pl
from jax.experimental.pallas import tpu as pltpu

B = 4096
STEPS = 2

ridge_weight = 0.5
kernel_scale = 0.125
ALL = ("grp", "mem")
HIGHEST = lax.Precision.HIGHEST
HIGH = lax.Precision.HIGH


def gather_all(piece, n_dev):
    sent = jnp.broadcast_to(piece[None], (n_dev,) + piece.shape)
    return lax.all_to_all(sent, ALL, 0, 0, tiled=True)


def split3(x):
    x1 = lax.reduce_precision(x, exponent_bits=8, mantissa_bits=7)
    r1 = x - x1
    x2 = lax.reduce_precision(r1, exponent_bits=8, mantissa_bits=7)
    r2 = r1 - x2
    return x1.astype(jnp.bfloat16), x2.astype(jnp.bfloat16), r2.astype(jnp.bfloat16)


def kern(u, v):
    nu = jnp.sum(u * u, axis=0, keepdims=True)
    nv = jnp.sum(v * v, axis=0, keepdims=True)
    u1, u2, u3 = split3(u)
    v1, v2, v3 = split3(-2.0 * v)
    a1, a2, a3 = split3(nu)
    b1, b2, b3 = split3(nv)
    one_u = jnp.ones_like(a1)
    one_v = jnp.ones_like(b1)
    left = jnp.concatenate([u1, u1, u2, u1, u3, u2, a1, a2, a3, one_u, one_u, one_u], axis=0)
    right = jnp.concatenate([v1, v2, v1, v3, v1, v2, one_v, one_v, one_v, b1, b2, b3], axis=0)
    dist = lax.dot_general(left, right, (((0,), (0,)), ((), ())), preferred_element_type=jnp.float32)
    kernel = jnp.exp(-kernel_scale * dist)
    k1 = lax.reduce_precision(kernel, exponent_bits=8, mantissa_bits=7)
    return lax.optimization_barrier((k1.astype(jnp.bfloat16), (kernel - k1).astype(jnp.bfloat16)))


def product_kernel(k1_ref, k2_ref, d12_ref, d1_ref, o_ref):
    both = jnp.dot(k1_ref[...], d12_ref[...], preferred_element_type=jnp.float32)
    low = jnp.dot(k2_ref[...], d1_ref[...], preferred_element_type=jnp.float32)
    rows = o_ref.shape[1]
    o_ref[...] = (both[:, :rows] + both[:, rows:]) + low


def apply_kernel(delta, kernel, tile=256):
    k1, k2 = kernel
    n, m = k1.shape
    rows = delta.shape[0]
    d1f = lax.reduce_precision(delta, exponent_bits=8, mantissa_bits=7)
    d1 = d1f.astype(jnp.bfloat16)
    d2 = (delta - d1f).astype(jnp.bfloat16)
    d12 = jnp.concatenate([d1, d2], axis=0).T
    tile = min(tile, n)
    out = pl.pallas_call(
        product_kernel,
        grid=(n // tile,),
        in_specs=[
            pl.BlockSpec((tile, m), lambda i: (i, 0)),
            pl.BlockSpec((tile, m), lambda i: (i, 0)),
            pl.BlockSpec((m, 2 * rows), lambda i: (0, 0)),
            pl.BlockSpec((m, rows), lambda i: (0, 0)),
        ],
        out_specs=pl.BlockSpec((tile, rows), lambda i: (i, 0)),
        out_shape=jax.ShapeDtypeStruct((n, rows), jnp.float32),
        compiler_params=pltpu.CompilerParams(vmem_limit_bytes=48 * 1024 * 1024),
        cost_estimate=pl.CostEstimate(
            flops=6 * rows * n * m, transcendentals=0, bytes_accessed=4 * n * m + 6 * m * rows
        ),
    )(k1, k2, d12, d1.T)
    return out.T


def exact_dot(x, onehot, dims):
    rows = x.shape[0]
    parts = jnp.concatenate(split3(x), axis=0)
    out = lax.dot_general(parts, onehot, dims, preferred_element_type=jnp.float32)
    return (out[:rows] + out[rows:2 * rows]) + out[2 * rows:]


def solve_kernel(slot_ref, inv_ref, rcat_ref, r1_ref, o_ref):
    a = inv_ref[...]
    hi = a.astype(jnp.bfloat16)
    lo = (a - hi.astype(jnp.float32)).astype(jnp.bfloat16)
    dims = (((1,), (1,)), ((), ()))
    both = lax.dot_general(rcat_ref[...], hi, dims, preferred_element_type=jnp.float32)
    low = lax.dot_general(r1_ref[...], lo, dims, preferred_element_type=jnp.float32)
    rows = o_ref.shape[0]
    o_ref[...] = (both[:rows] + both[rows:]) + low


def solve_rows(inverse, slot, block_res, tile=256):
    _, n, width = inverse.shape
    rows = block_res.shape[0]
    r1f = lax.reduce_precision(block_res, exponent_bits=8, mantissa_bits=7)
    r1 = r1f.astype(jnp.bfloat16)
    r2 = (block_res - r1f).astype(jnp.bfloat16)
    rcat = jnp.concatenate([r1, r2], axis=0)
    tile = min(tile, n)
    grid_spec = pltpu.PrefetchScalarGridSpec(
        num_scalar_prefetch=1,
        grid=(n // tile,),
        in_specs=[
            pl.BlockSpec((None, tile, width), lambda i, s: (s[0], i, 0)),
            pl.BlockSpec((2 * rows, width), lambda i, s: (0, 0)),
            pl.BlockSpec((rows, width), lambda i, s: (0, 0)),
        ],
        out_specs=pl.BlockSpec((rows, tile), lambda i, s: (0, i)),
    )
    return pl.pallas_call(
        solve_kernel,
        grid_spec=grid_spec,
        out_shape=jax.ShapeDtypeStruct((rows, n), jnp.float32),
        compiler_params=pltpu.CompilerParams(vmem_limit_bytes=48 * 1024 * 1024),
        cost_estimate=pl.CostEstimate(
            flops=6 * rows * n * width, transcendentals=0, bytes_accessed=4 * n * width
        ),
    )(jnp.reshape(slot, (1,)).astype(jnp.int32), inverse, rcat, r1)


def body(points, residual, coef, block_of, order, inverse):
    n_grp = lax.axis_size("grp")
    n_mem = lax.axis_size("mem")
    n_dev = n_grp * n_mem
    per = B // n_dev
    slots = inverse.shape[0]
    feat = points.shape[0]
    rhs = residual.shape[0]
    mine = lax.axis_index("grp") * n_mem + lax.axis_index("mem")

    def selector(block_id):
        inside = block_of == block_id
        position = jnp.cumsum(inside.astype(jnp.int32)) - 1
        return (
            (position[:, None] == jnp.arange(per, dtype=jnp.int32)[None, :]) & inside[:, None]
        ).astype(jnp.bfloat16)

    def solve(block_res, block_id):
        return distribute(solve_rows(inverse, block_id % slots, block_res), block_id)

    def distribute(solved, block_id):
        owner = block_id // slots
        pieces = jnp.transpose(solved.reshape(rhs, n_grp, per), (1, 0, 2))
        scattered = lax.all_to_all(pieces, "grp", 0, 0, tiled=True)
        piece = lax.dynamic_index_in_dim(scattered, owner, 0, keepdims=False)
        pieces_all = gather_all(piece, n_dev)
        pieces_all = jnp.transpose(pieces_all.reshape(n_grp, n_mem, rhs, per), (2, 1, 0, 3))
        return pieces_all.reshape(rhs, B)

    def to_block(gathered, rows):
        return jnp.transpose(gathered, (1, 0, 2)).reshape(rows, B)

    block0, block1 = order[0], order[1]
    sel0 = selector(block0)
    sel1 = selector(block1)
    plain = (((1,), (0,)), ((), ()))
    chosen = exact_dot(
        jnp.concatenate([residual, points], axis=0), jnp.concatenate([sel0, sel1], axis=1), plain
    )
    chosen0 = chosen[:, :per]
    res1_start = chosen[:rhs, per:]
    pts1_local = chosen[rhs:, per:]
    gathered = to_block(gather_all(jnp.concatenate([chosen0, pts1_local], axis=0), n_dev), rhs + 2 * feat)
    block_res0 = gathered[:rhs]
    block_pts0 = gathered[rhs:rhs + feat]
    block_pts1 = gathered[rhs + feat:]

    delta0 = solve(block_res0, block0)
    owned0 = lax.dynamic_slice_in_dim(delta0, mine * per, per, axis=1)
    early = apply_kernel(delta0, kern(pts1_local, block_pts0))
    overlap = lax.dot_general(sel0, sel1, (((0,), (0,)), ((), ())), preferred_element_type=jnp.float32)
    overlap = overlap.astype(jnp.bfloat16)
    res1_local = res1_start - early - ridge_weight * exact_dot(owned0, overlap, plain)
    res1_local, pts_late, pts1_late = lax.optimization_barrier((res1_local, points, block_pts1))
    block_res1 = to_block(gather_all(res1_local, n_dev), rhs)
    kernel1 = kern(pts_late, pts1_late)

    solved1 = solve_rows(inverse, block1 % slots, block_res1)
    solved1, pts_later, pts0_later = lax.optimization_barrier((solved1, points, block_pts0))
    delta1 = distribute(solved1, block1)
    spread0 = exact_dot(owned0, sel0, (((1,), (1,)), ((), ())))
    update0 = apply_kernel(delta0, kern(pts_later, pts0_later))
    residual = residual - update0 - ridge_weight * spread0
    coef = coef + spread0

    owned1 = lax.dynamic_slice_in_dim(delta1, mine * per, per, axis=1)
    spread1 = exact_dot(owned1, sel1, (((1,), (1,)), ((), ())))
    update1 = apply_kernel(delta1, kernel1)
    residual = residual - update1 - ridge_weight * spread1
    coef = coef + spread1
    return (residual, coef)


def solution(mesh):
    in_specs = (
        P(None, ("grp", "mem")),
        P(None, ("grp", "mem")),
        P(None, ("grp", "mem")),
        P(("grp", "mem")),
        P(),
        P("grp", "mem", None),
    )
    out_specs = (P(None, ("grp", "mem")), P(None, ("grp", "mem")))
    return jax.shard_map(body, mesh=mesh, in_specs=in_specs, out_specs=out_specs, check_vma=False)
```

```python
import jax
import jax.numpy as jnp
from jax import lax
from jax.sharding import PartitionSpec as P
from jax.experimental import pallas as pl
from jax.experimental.pallas import tpu as pltpu

B = 4096
STEPS = 2

ridge_weight = 0.5
kernel_scale = 0.125
ALL = ("grp", "mem")
HIGHEST = lax.Precision.HIGHEST
HIGH = lax.Precision.HIGH


def gather_all(piece, n_dev):
    sent = jnp.broadcast_to(piece[None], (n_dev,) + piece.shape)
    return lax.all_to_all(sent, ALL, 0, 0, tiled=True)


def split3(x):
    x1 = lax.reduce_precision(x, exponent_bits=8, mantissa_bits=7)
    r1 = x - x1
    x2 = lax.reduce_precision(r1, exponent_bits=8, mantissa_bits=7)
    r2 = r1 - x2
    return x1.astype(jnp.bfloat16), x2.astype(jnp.bfloat16), r2.astype(jnp.bfloat16)


def kern(u, v):
    nu = jnp.sum(u * u, axis=0)
    nv = jnp.sum(v * v, axis=0)
    u1, u2, u3 = split3(u)
    v1, v2, v3 = split3(-2.0 * v)
    left = jnp.concatenate([u1, u1, u2, u1, u3, u2], axis=0)
    right = jnp.concatenate([v1, v2, v1, v3, v1, v2], axis=0)
    cross2 = lax.dot_general(left, right, (((0,), (0,)), ((), ())), preferred_element_type=jnp.float32)
    kernel = jnp.exp(-kernel_scale * ((nu[:, None] + nv[None, :]) + cross2))
    k1 = lax.reduce_precision(kernel, exponent_bits=8, mantissa_bits=7)
    return lax.optimization_barrier((k1.astype(jnp.bfloat16), (kernel - k1).astype(jnp.bfloat16)))


def apply_kernel(delta, kernel):
    k1, k2 = kernel
    d1f = lax.reduce_precision(delta, exponent_bits=8, mantissa_bits=7)
    d1 = d1f.astype(jnp.bfloat16)
    d2 = (delta - d1f).astype(jnp.bfloat16)
    rows = delta.shape[0]
    dims = (((1,), (1,)), ((), ()))
    both = lax.dot_general(jnp.concatenate([d1, d2], axis=0), k1, dims, preferred_element_type=jnp.float32)
    low = lax.dot_general(d1, k2, dims, preferred_element_type=jnp.float32)
    return (both[:rows] + both[rows:]) + low


def exact_dot(x, onehot, dims):
    rows = x.shape[0]
    parts = jnp.concatenate(split3(x), axis=0)
    out = lax.dot_general(parts, onehot, dims, preferred_element_type=jnp.float32)
    return (out[:rows] + out[rows:2 * rows]) + out[2 * rows:]


def solve_kernel(slot_ref, inv_ref, rcat_ref, r1_ref, o_ref):
    a = inv_ref[...]
    hi = a.astype(jnp.bfloat16)
    lo = (a - hi.astype(jnp.float32)).astype(jnp.bfloat16)
    dims = (((1,), (1,)), ((), ()))
    both = lax.dot_general(rcat_ref[...], hi, dims, preferred_element_type=jnp.float32)
    low = lax.dot_general(r1_ref[...], lo, dims, preferred_element_type=jnp.float32)
    rows = o_ref.shape[0]
    o_ref[...] = (both[:rows] + both[rows:]) + low


def solve_rows(inverse, slot, block_res, tile=256):
    _, n, width = inverse.shape
    rows = block_res.shape[0]
    r1f = lax.reduce_precision(block_res, exponent_bits=8, mantissa_bits=7)
    r1 = r1f.astype(jnp.bfloat16)
    r2 = (block_res - r1f).astype(jnp.bfloat16)
    rcat = jnp.concatenate([r1, r2], axis=0)
    tile = min(tile, n)
    grid_spec = pltpu.PrefetchScalarGridSpec(
        num_scalar_prefetch=1,
        grid=(n // tile,),
        in_specs=[
            pl.BlockSpec((None, tile, width), lambda i, s: (s[0], i, 0)),
            pl.BlockSpec((2 * rows, width), lambda i, s: (0, 0)),
            pl.BlockSpec((rows, width), lambda i, s: (0, 0)),
        ],
        out_specs=pl.BlockSpec((rows, tile), lambda i, s: (0, i)),
    )
    return pl.pallas_call(
        solve_kernel,
        grid_spec=grid_spec,
        out_shape=jax.ShapeDtypeStruct((rows, n), jnp.float32),
        compiler_params=pltpu.CompilerParams(vmem_limit_bytes=48 * 1024 * 1024),
        cost_estimate=pl.CostEstimate(
            flops=6 * rows * n * width, transcendentals=0, bytes_accessed=4 * n * width
        ),
    )(jnp.reshape(slot, (1,)).astype(jnp.int32), inverse, rcat, r1)


def body(points, residual, coef, block_of, order, inverse):
    n_grp = lax.axis_size("grp")
    n_mem = lax.axis_size("mem")
    n_dev = n_grp * n_mem
    per = B // n_dev
    slots = inverse.shape[0]
    feat = points.shape[0]
    rhs = residual.shape[0]
    mine = lax.axis_index("grp") * n_mem + lax.axis_index("mem")

    def selector(block_id):
        inside = block_of == block_id
        position = jnp.cumsum(inside.astype(jnp.int32)) - 1
        return (
            (position[:, None] == jnp.arange(per, dtype=jnp.int32)[None, :]) & inside[:, None]
        ).astype(jnp.bfloat16)

    def solve(block_res, block_id):
        return distribute(solve_rows(inverse, block_id % slots, block_res), block_id)

    def distribute(solved, block_id):
        owner = block_id // slots
        pieces = jnp.transpose(solved.reshape(rhs, n_grp, per), (1, 0, 2))
        scattered = lax.all_to_all(pieces, "grp", 0, 0, tiled=True)
        piece = lax.dynamic_index_in_dim(scattered, owner, 0, keepdims=False)
        pieces_all = gather_all(piece, n_dev)
        pieces_all = jnp.transpose(pieces_all.reshape(n_grp, n_mem, rhs, per), (2, 1, 0, 3))
        return pieces_all.reshape(rhs, B)

    def to_block(gathered, rows):
        return jnp.transpose(gathered, (1, 0, 2)).reshape(rows, B)

    block0, block1 = order[0], order[1]
    sel0 = selector(block0)
    sel1 = selector(block1)
    plain = (((1,), (0,)), ((), ()))
    chosen = exact_dot(
        jnp.concatenate([residual, points], axis=0), jnp.concatenate([sel0, sel1], axis=1), plain
    )
    chosen0 = chosen[:, :per]
    res1_start = chosen[:rhs, per:]
    pts1_local = chosen[rhs:, per:]
    gathered = to_block(gather_all(jnp.concatenate([chosen0, pts1_local], axis=0), n_dev), rhs + 2 * feat)
    block_res0 = gathered[:rhs]
    block_pts0 = gathered[rhs:rhs + feat]
    block_pts1 = gathered[rhs + feat:]

    delta0 = solve(block_res0, block0)
    owned0 = lax.dynamic_slice_in_dim(delta0, mine * per, per, axis=1)
    early = apply_kernel(delta0, kern(pts1_local, block_pts0))
    overlap = lax.dot_general(sel0, sel1, (((0,), (0,)), ((), ())), preferred_element_type=jnp.float32)
    overlap = overlap.astype(jnp.bfloat16)
    res1_local = res1_start - early - ridge_weight * exact_dot(owned0, overlap, plain)
    res1_local, pts_late, pts1_late = lax.optimization_barrier((res1_local, points, block_pts1))
    block_res1 = to_block(gather_all(res1_local, n_dev), rhs)
    kernel1 = kern(pts_late, pts1_late)

    solved1 = solve_rows(inverse, block1 % slots, block_res1)
    solved1, pts_later, pts0_later = lax.optimization_barrier((solved1, points, block_pts0))
    delta1 = distribute(solved1, block1)
    spread0 = exact_dot(owned0, sel0, (((1,), (1,)), ((), ())))
    update0 = apply_kernel(delta0, kern(pts_later, pts0_later))
    residual = residual - update0 - ridge_weight * spread0
    coef = coef + spread0

    owned1 = lax.dynamic_slice_in_dim(delta1, mine * per, per, axis=1)
    spread1 = exact_dot(owned1, sel1, (((1,), (1,)), ((), ())))
    update1 = apply_kernel(delta1, kernel1)
    residual = residual - update1 - ridge_weight * spread1
    coef = coef + spread1
    return (residual, coef)


def solution(mesh):
    in_specs = (
        P(None, ("grp", "mem")),
        P(None, ("grp", "mem")),
        P(None, ("grp", "mem")),
        P(("grp", "mem")),
        P(),
        P("grp", "mem", None),
    )
    out_specs = (P(None, ("grp", "mem")), P(None, ("grp", "mem")))
    return jax.shard_map(body, mesh=mesh, in_specs=in_specs, out_specs=out_specs, check_vma=False)
```

```python
import jax
import jax.numpy as jnp
from jax import lax
from jax.sharding import PartitionSpec as P
from jax.experimental import pallas as pl
from jax.experimental.pallas import tpu as pltpu

B = 4096
STEPS = 2

ridge_weight = 0.5
kernel_scale = 0.125
ALL = ("grp", "mem")
HIGHEST = lax.Precision.HIGHEST
HIGH = lax.Precision.HIGH


def gather_all(piece, n_dev):
    sent = jnp.broadcast_to(piece[None], (n_dev,) + piece.shape)
    return lax.all_to_all(sent, ALL, 0, 0, tiled=True)


def split3(x):
    x1 = lax.reduce_precision(x, exponent_bits=8, mantissa_bits=7)
    r1 = x - x1
    x2 = lax.reduce_precision(r1, exponent_bits=8, mantissa_bits=7)
    r2 = r1 - x2
    return x1.astype(jnp.bfloat16), x2.astype(jnp.bfloat16), r2.astype(jnp.bfloat16)


def kern(u, v):
    nu = jnp.sum(u * u, axis=0)
    nv = jnp.sum(v * v, axis=0)
    u1, u2, u3 = split3(u)
    v1, v2, v3 = split3(-2.0 * v)
    left = jnp.concatenate([u1, u1, u2, u1, u3, u2], axis=0)
    right = jnp.concatenate([v1, v2, v1, v3, v1, v2], axis=0)
    cross2 = lax.dot_general(left, right, (((0,), (0,)), ((), ())), preferred_element_type=jnp.float32)
    kernel = jnp.exp(-kernel_scale * ((nu[:, None] + nv[None, :]) + cross2))
    k1 = lax.reduce_precision(kernel, exponent_bits=8, mantissa_bits=7)
    return lax.optimization_barrier((k1.astype(jnp.bfloat16), (kernel - k1).astype(jnp.bfloat16)))


def apply_kernel(delta, kernel):
    k1, k2 = kernel
    d1f = lax.reduce_precision(delta, exponent_bits=8, mantissa_bits=7)
    d1 = d1f.astype(jnp.bfloat16)
    d2 = (delta - d1f).astype(jnp.bfloat16)
    rows = delta.shape[0]
    dims = (((1,), (1,)), ((), ()))
    both = lax.dot_general(jnp.concatenate([d1, d2], axis=0), k1, dims, preferred_element_type=jnp.float32)
    low = lax.dot_general(d1, k2, dims, preferred_element_type=jnp.float32)
    return (both[:rows] + both[rows:]) + low


def exact_dot(x, onehot, dims):
    rows = x.shape[0]
    parts = jnp.concatenate(split3(x), axis=0)
    out = lax.dot_general(parts, onehot, dims, preferred_element_type=jnp.float32)
    return (out[:rows] + out[rows:2 * rows]) + out[2 * rows:]


def solve_kernel(slot_ref, inv_ref, rcat_ref, r1_ref, o_ref):
    a = inv_ref[...]
    hi = a.astype(jnp.bfloat16)
    lo = (a - hi.astype(jnp.float32)).astype(jnp.bfloat16)
    dims = (((1,), (1,)), ((), ()))
    both = lax.dot_general(rcat_ref[...], hi, dims, preferred_element_type=jnp.float32)
    low = lax.dot_general(r1_ref[...], lo, dims, preferred_element_type=jnp.float32)
    rows = o_ref.shape[0]
    o_ref[...] = (both[:rows] + both[rows:]) + low


def solve_rows(inverse, slot, block_res, tile=256):
    _, n, width = inverse.shape
    rows = block_res.shape[0]
    r1f = lax.reduce_precision(block_res, exponent_bits=8, mantissa_bits=7)
    r1 = r1f.astype(jnp.bfloat16)
    r2 = (block_res - r1f).astype(jnp.bfloat16)
    rcat = jnp.concatenate([r1, r2], axis=0)
    tile = min(tile, n)
    grid_spec = pltpu.PrefetchScalarGridSpec(
        num_scalar_prefetch=1,
        grid=(n // tile,),
        in_specs=[
            pl.BlockSpec((None, tile, width), lambda i, s: (s[0], i, 0)),
            pl.BlockSpec((2 * rows, width), lambda i, s: (0, 0)),
            pl.BlockSpec((rows, width), lambda i, s: (0, 0)),
        ],
        out_specs=pl.BlockSpec((rows, tile), lambda i, s: (0, i)),
    )
    return pl.pallas_call(
        solve_kernel,
        grid_spec=grid_spec,
        out_shape=jax.ShapeDtypeStruct((rows, n), jnp.float32),
        compiler_params=pltpu.CompilerParams(vmem_limit_bytes=48 * 1024 * 1024),
        cost_estimate=pl.CostEstimate(
            flops=6 * rows * n * width, transcendentals=0, bytes_accessed=4 * n * width
        ),
    )(jnp.reshape(slot, (1,)).astype(jnp.int32), inverse, rcat, r1)


def body(points, residual, coef, block_of, order, inverse):
    n_grp = lax.axis_size("grp")
    n_mem = lax.axis_size("mem")
    n_dev = n_grp * n_mem
    per = B // n_dev
    slots = inverse.shape[0]
    feat = points.shape[0]
    rhs = residual.shape[0]
    mine = lax.axis_index("grp") * n_mem + lax.axis_index("mem")

    def selector(block_id):
        inside = block_of == block_id
        position = jnp.cumsum(inside.astype(jnp.int32)) - 1
        return (
            (position[:, None] == jnp.arange(per, dtype=jnp.int32)[None, :]) & inside[:, None]
        ).astype(jnp.bfloat16)

    def solve(block_res, block_id):
        return distribute(solve_rows(inverse, block_id % slots, block_res), block_id)

    def distribute(solved, block_id):
        owner = block_id // slots
        pieces = jnp.transpose(solved.reshape(rhs, n_grp, per), (1, 0, 2))
        scattered = lax.all_to_all(pieces, "grp", 0, 0, tiled=True)
        piece = lax.dynamic_index_in_dim(scattered, owner, 0, keepdims=False)
        pieces_all = gather_all(piece, n_dev)
        pieces_all = jnp.transpose(pieces_all.reshape(n_grp, n_mem, rhs, per), (2, 1, 0, 3))
        return pieces_all.reshape(rhs, B)

    def to_block(gathered, rows):
        return jnp.transpose(gathered, (1, 0, 2)).reshape(rows, B)

    block0, block1 = order[0], order[1]
    sel0 = selector(block0)
    sel1 = selector(block1)
    plain = (((1,), (0,)), ((), ()))
    chosen = exact_dot(
        jnp.concatenate([residual, points], axis=0), jnp.concatenate([sel0, sel1], axis=1), plain
    )
    chosen0 = chosen[:, :per]
    res1_start = chosen[:rhs, per:]
    pts1_local = chosen[rhs:, per:]
    gathered = to_block(gather_all(jnp.concatenate([chosen0, pts1_local], axis=0), n_dev), rhs + 2 * feat)
    block_res0 = gathered[:rhs]
    block_pts0 = gathered[rhs:rhs + feat]
    block_pts1 = gathered[rhs + feat:]

    delta0 = solve(block_res0, block0)
    owned0 = lax.dynamic_slice_in_dim(delta0, mine * per, per, axis=1)
    kernel0 = kern(points, block_pts0)
    early = apply_kernel(delta0, kern(pts1_local, block_pts0))
    overlap = lax.dot_general(sel0, sel1, (((0,), (0,)), ((), ())), preferred_element_type=jnp.float32)
    overlap = overlap.astype(jnp.bfloat16)
    res1_local = res1_start - early - ridge_weight * exact_dot(owned0, overlap, plain)
    res1_local, pts_late, pts1_late = lax.optimization_barrier((res1_local, points, block_pts1))
    block_res1 = to_block(gather_all(res1_local, n_dev), rhs)
    kernel1 = kern(pts_late, pts1_late)

    solved1 = solve_rows(inverse, block1 % slots, block_res1)
    solved1, delta0_late = lax.optimization_barrier((solved1, delta0))
    delta1 = distribute(solved1, block1)
    spread0 = exact_dot(owned0, sel0, (((1,), (1,)), ((), ())))
    update0 = apply_kernel(delta0_late, kernel0)
    residual = residual - update0 - ridge_weight * spread0
    coef = coef + spread0

    owned1 = lax.dynamic_slice_in_dim(delta1, mine * per, per, axis=1)
    spread1 = exact_dot(owned1, sel1, (((1,), (1,)), ((), ())))
    update1 = apply_kernel(delta1, kernel1)
    residual = residual - update1 - ridge_weight * spread1
    coef = coef + spread1
    return (residual, coef)


def solution(mesh):
    in_specs = (
        P(None, ("grp", "mem")),
        P(None, ("grp", "mem")),
        P(None, ("grp", "mem")),
        P(("grp", "mem")),
        P(),
        P("grp", "mem", None),
    )
    out_specs = (P(None, ("grp", "mem")), P(None, ("grp", "mem")))
    return jax.shard_map(body, mesh=mesh, in_specs=in_specs, out_specs=out_specs, check_vma=False)
```

```python
import jax
import jax.numpy as jnp
from jax import lax
from jax.sharding import PartitionSpec as P
from jax.experimental import pallas as pl
from jax.experimental.pallas import tpu as pltpu

B = 4096
STEPS = 2

ridge_weight = 0.5
kernel_scale = 0.125
ALL = ("grp", "mem")
HIGHEST = lax.Precision.HIGHEST
HIGH = lax.Precision.HIGH


def gather_all(piece, n_dev):
    sent = jnp.broadcast_to(piece[None], (n_dev,) + piece.shape)
    return lax.all_to_all(sent, ALL, 0, 0, tiled=True)


def split3(x):
    x1 = lax.reduce_precision(x, exponent_bits=8, mantissa_bits=7)
    r1 = x - x1
    x2 = lax.reduce_precision(r1, exponent_bits=8, mantissa_bits=7)
    r2 = r1 - x2
    return x1.astype(jnp.bfloat16), x2.astype(jnp.bfloat16), r2.astype(jnp.bfloat16)


def kern(u, v):
    nu = jnp.sum(u * u, axis=0)
    nv = jnp.sum(v * v, axis=0)
    u1, u2, u3 = split3(u)
    v1, v2, v3 = split3(-2.0 * v)
    left = jnp.concatenate([u1, u1, u2, u1, u3, u2], axis=0)
    right = jnp.concatenate([v1, v2, v1, v3, v1, v2], axis=0)
    cross2 = lax.dot_general(left, right, (((0,), (0,)), ((), ())), preferred_element_type=jnp.float32)
    kernel = jnp.exp(-kernel_scale * ((nu[:, None] + nv[None, :]) + cross2))
    k1 = lax.reduce_precision(kernel, exponent_bits=8, mantissa_bits=7)
    return lax.optimization_barrier((k1.astype(jnp.bfloat16), (kernel - k1).astype(jnp.bfloat16)))


def apply_kernel(delta, kernel):
    k1, k2 = kernel
    d1f = lax.reduce_precision(delta, exponent_bits=8, mantissa_bits=7)
    d1 = d1f.astype(jnp.bfloat16)
    d2 = (delta - d1f).astype(jnp.bfloat16)
    rows = delta.shape[0]
    dims = (((1,), (1,)), ((), ()))
    both = lax.dot_general(jnp.concatenate([d1, d2], axis=0), k1, dims, preferred_element_type=jnp.float32)
    low = lax.dot_general(d1, k2, dims, preferred_element_type=jnp.float32)
    return (both[:rows] + both[rows:]) + low


def exact_dot(x, onehot, dims):
    rows = x.shape[0]
    parts = jnp.concatenate(split3(x), axis=0)
    out = lax.dot_general(parts, onehot, dims, preferred_element_type=jnp.float32)
    return (out[:rows] + out[rows:2 * rows]) + out[2 * rows:]


def solve_kernel(slot_ref, inv_ref, rcat_ref, r1_ref, o_ref):
    a = inv_ref[...]
    hi = a.astype(jnp.bfloat16)
    lo = (a - hi.astype(jnp.float32)).astype(jnp.bfloat16)
    dims = (((1,), (1,)), ((), ()))
    both = lax.dot_general(rcat_ref[...], hi, dims, preferred_element_type=jnp.float32)
    low = lax.dot_general(r1_ref[...], lo, dims, preferred_element_type=jnp.float32)
    rows = o_ref.shape[0]
    o_ref[...] = (both[:rows] + both[rows:]) + low


def solve_rows(inverse, slot, block_res, tile=256):
    _, n, width = inverse.shape
    rows = block_res.shape[0]
    r1f = lax.reduce_precision(block_res, exponent_bits=8, mantissa_bits=7)
    r1 = r1f.astype(jnp.bfloat16)
    r2 = (block_res - r1f).astype(jnp.bfloat16)
    rcat = jnp.concatenate([r1, r2], axis=0)
    tile = min(tile, n)
    grid_spec = pltpu.PrefetchScalarGridSpec(
        num_scalar_prefetch=1,
        grid=(n // tile,),
        in_specs=[
            pl.BlockSpec((None, tile, width), lambda i, s: (s[0], i, 0)),
            pl.BlockSpec((2 * rows, width), lambda i, s: (0, 0)),
            pl.BlockSpec((rows, width), lambda i, s: (0, 0)),
        ],
        out_specs=pl.BlockSpec((rows, tile), lambda i, s: (0, i)),
    )
    return pl.pallas_call(
        solve_kernel,
        grid_spec=grid_spec,
        out_shape=jax.ShapeDtypeStruct((rows, n), jnp.float32),
        compiler_params=pltpu.CompilerParams(vmem_limit_bytes=48 * 1024 * 1024),
        cost_estimate=pl.CostEstimate(
            flops=6 * rows * n * width, transcendentals=0, bytes_accessed=4 * n * width
        ),
    )(jnp.reshape(slot, (1,)).astype(jnp.int32), inverse, rcat, r1)


def body(points, residual, coef, block_of, order, inverse):
    n_grp = lax.axis_size("grp")
    n_mem = lax.axis_size("mem")
    n_dev = n_grp * n_mem
    per = B // n_dev
    slots = inverse.shape[0]
    feat = points.shape[0]
    rhs = residual.shape[0]
    mine = lax.axis_index("grp") * n_mem + lax.axis_index("mem")

    def selector(block_id):
        inside = block_of == block_id
        position = jnp.cumsum(inside.astype(jnp.int32)) - 1
        return (
            (position[:, None] == jnp.arange(per, dtype=jnp.int32)[None, :]) & inside[:, None]
        ).astype(jnp.bfloat16)

    def solve(block_res, block_id):
        return distribute(solve_rows(inverse, block_id % slots, block_res), block_id)

    def distribute(solved, block_id):
        owner = block_id // slots
        pieces = jnp.transpose(solved.reshape(rhs, n_grp, per), (1, 0, 2))
        scattered = lax.all_to_all(pieces, "grp", 0, 0, tiled=True)
        piece = lax.dynamic_index_in_dim(scattered, owner, 0, keepdims=False)
        pieces_all = gather_all(piece, n_dev)
        pieces_all = jnp.transpose(pieces_all.reshape(n_grp, n_mem, rhs, per), (2, 1, 0, 3))
        return pieces_all.reshape(rhs, B)

    def to_block(gathered, rows):
        return jnp.transpose(gathered, (1, 0, 2)).reshape(rows, B)

    block0, block1 = order[0], order[1]
    sel0 = selector(block0)
    sel1 = selector(block1)
    plain = (((1,), (0,)), ((), ()))
    chosen = exact_dot(
        jnp.concatenate([residual, points], axis=0), jnp.concatenate([sel0, sel1], axis=1), plain
    )
    chosen0 = chosen[:, :per]
    res1_start = chosen[:rhs, per:]
    pts1_local = chosen[rhs:, per:]
    block_res0 = to_block(gather_all(chosen0[:rhs], n_dev), rhs)
    gathered = to_block(gather_all(jnp.concatenate([chosen0[rhs:], pts1_local], axis=0), n_dev), 2 * feat)
    block_pts0 = gathered[:feat]
    block_pts1 = gathered[feat:]

    delta0 = solve(block_res0, block0)
    owned0 = lax.dynamic_slice_in_dim(delta0, mine * per, per, axis=1)
    kernel0 = kern(points, block_pts0)
    early = apply_kernel(delta0, kern(pts1_local, block_pts0))
    overlap = lax.dot_general(sel0, sel1, (((0,), (0,)), ((), ())), preferred_element_type=jnp.float32)
    overlap = overlap.astype(jnp.bfloat16)
    res1_local = res1_start - early - ridge_weight * exact_dot(owned0, overlap, plain)
    res1_local, pts_late, pts1_late = lax.optimization_barrier((res1_local, points, block_pts1))
    block_res1 = to_block(gather_all(res1_local, n_dev), rhs)
    kernel1 = kern(pts_late, pts1_late)

    solved1 = solve_rows(inverse, block1 % slots, block_res1)
    solved1, delta0_late = lax.optimization_barrier((solved1, delta0))
    delta1 = distribute(solved1, block1)
    spread0 = exact_dot(owned0, sel0, (((1,), (1,)), ((), ())))
    update0 = apply_kernel(delta0_late, kernel0)
    residual = residual - update0 - ridge_weight * spread0
    coef = coef + spread0

    owned1 = lax.dynamic_slice_in_dim(delta1, mine * per, per, axis=1)
    spread1 = exact_dot(owned1, sel1, (((1,), (1,)), ((), ())))
    update1 = apply_kernel(delta1, kernel1)
    residual = residual - update1 - ridge_weight * spread1
    coef = coef + spread1
    return (residual, coef)


def solution(mesh):
    in_specs = (
        P(None, ("grp", "mem")),
        P(None, ("grp", "mem")),
        P(None, ("grp", "mem")),
        P(("grp", "mem")),
        P(),
        P("grp", "mem", None),
    )
    out_specs = (P(None, ("grp", "mem")), P(None, ("grp", "mem")))
    return jax.shard_map(body, mesh=mesh, in_specs=in_specs, out_specs=out_specs, check_vma=False)
```

```python
import jax
import jax.numpy as jnp
from jax import lax
from jax.sharding import PartitionSpec as P
from jax.experimental import pallas as pl
from jax.experimental.pallas import tpu as pltpu

B = 4096
STEPS = 2

ridge_weight = 0.5
kernel_scale = 0.125
ALL = ("grp", "mem")
HIGHEST = lax.Precision.HIGHEST
HIGH = lax.Precision.HIGH


def gather_all(piece, n_dev):
    sent = jnp.broadcast_to(piece[None], (n_dev,) + piece.shape)
    return lax.all_to_all(sent, ALL, 0, 0, tiled=True)


def split3(x):
    x1 = lax.reduce_precision(x, exponent_bits=8, mantissa_bits=7)
    r1 = x - x1
    x2 = lax.reduce_precision(r1, exponent_bits=8, mantissa_bits=7)
    r2 = r1 - x2
    return x1.astype(jnp.bfloat16), x2.astype(jnp.bfloat16), r2.astype(jnp.bfloat16)


def kern(u, v):
    nu = jnp.sum(u * u, axis=0)
    nv = jnp.sum(v * v, axis=0)
    u1, u2, u3 = split3(u)
    v1, v2, v3 = split3(-2.0 * v)
    left = jnp.concatenate([u1, u1, u2, u1, u3, u2], axis=0)
    right = jnp.concatenate([v1, v2, v1, v3, v1, v2], axis=0)
    cross2 = lax.dot_general(left, right, (((0,), (0,)), ((), ())), preferred_element_type=jnp.float32)
    kernel = jnp.exp(-kernel_scale * ((nu[:, None] + nv[None, :]) + cross2))
    k1 = lax.reduce_precision(kernel, exponent_bits=8, mantissa_bits=7)
    return lax.optimization_barrier((k1.astype(jnp.bfloat16), (kernel - k1).astype(jnp.bfloat16)))


def apply_kernel(delta, kernel):
    k1, k2 = kernel
    d1f = lax.reduce_precision(delta, exponent_bits=8, mantissa_bits=7)
    d1 = d1f.astype(jnp.bfloat16)
    d2 = (delta - d1f).astype(jnp.bfloat16)
    rows = delta.shape[0]
    dims = (((1,), (1,)), ((), ()))
    both = lax.dot_general(jnp.concatenate([d1, d2], axis=0), k1, dims, preferred_element_type=jnp.float32)
    low = lax.dot_general(d1, k2, dims, preferred_element_type=jnp.float32)
    return (both[:rows] + both[rows:]) + low


def exact_dot(x, onehot, dims):
    rows = x.shape[0]
    parts = jnp.concatenate(split3(x), axis=0)
    out = lax.dot_general(parts, onehot, dims, preferred_element_type=jnp.float32)
    return (out[:rows] + out[rows:2 * rows]) + out[2 * rows:]


def solve_kernel(slot_ref, inv_ref, rcat_ref, r1_ref, o_ref):
    a = inv_ref[...]
    hi = a.astype(jnp.bfloat16)
    lo = (a - hi.astype(jnp.float32)).astype(jnp.bfloat16)
    dims = (((1,), (1,)), ((), ()))
    both = lax.dot_general(rcat_ref[...], hi, dims, preferred_element_type=jnp.float32)
    low = lax.dot_general(r1_ref[...], lo, dims, preferred_element_type=jnp.float32)
    rows = o_ref.shape[0]
    o_ref[...] = (both[:rows] + both[rows:]) + low


def solve_rows(inverse, slot, block_res, tile=128):
    _, n, width = inverse.shape
    rows = block_res.shape[0]
    r1f = lax.reduce_precision(block_res, exponent_bits=8, mantissa_bits=7)
    r1 = r1f.astype(jnp.bfloat16)
    r2 = (block_res - r1f).astype(jnp.bfloat16)
    rcat = jnp.concatenate([r1, r2], axis=0)
    tile = min(tile, n)
    grid_spec = pltpu.PrefetchScalarGridSpec(
        num_scalar_prefetch=1,
        grid=(n // tile,),
        in_specs=[
            pl.BlockSpec((None, tile, width), lambda i, s: (s[0], i, 0)),
            pl.BlockSpec((2 * rows, width), lambda i, s: (0, 0)),
            pl.BlockSpec((rows, width), lambda i, s: (0, 0)),
        ],
        out_specs=pl.BlockSpec((rows, tile), lambda i, s: (0, i)),
    )
    return pl.pallas_call(
        solve_kernel,
        grid_spec=grid_spec,
        out_shape=jax.ShapeDtypeStruct((rows, n), jnp.float32),
        compiler_params=pltpu.CompilerParams(vmem_limit_bytes=48 * 1024 * 1024),
        cost_estimate=pl.CostEstimate(
            flops=6 * rows * n * width, transcendentals=0, bytes_accessed=4 * n * width
        ),
    )(jnp.reshape(slot, (1,)).astype(jnp.int32), inverse, rcat, r1)


def body(points, residual, coef, block_of, order, inverse):
    n_grp = lax.axis_size("grp")
    n_mem = lax.axis_size("mem")
    n_dev = n_grp * n_mem
    per = B // n_dev
    slots = inverse.shape[0]
    feat = points.shape[0]
    rhs = residual.shape[0]
    mine = lax.axis_index("grp") * n_mem + lax.axis_index("mem")

    def selector(block_id):
        inside = block_of == block_id
        position = jnp.cumsum(inside.astype(jnp.int32)) - 1
        return (
            (position[:, None] == jnp.arange(per, dtype=jnp.int32)[None, :]) & inside[:, None]
        ).astype(jnp.bfloat16)

    def solve(block_res, block_id):
        return distribute(solve_rows(inverse, block_id % slots, block_res), block_id)

    def distribute(solved, block_id):
        owner = block_id // slots
        pieces = jnp.transpose(solved.reshape(rhs, n_grp, per), (1, 0, 2))
        scattered = lax.all_to_all(pieces, "grp", 0, 0, tiled=True)
        piece = lax.dynamic_index_in_dim(scattered, owner, 0, keepdims=False)
        pieces_all = gather_all(piece, n_dev)
        pieces_all = jnp.transpose(pieces_all.reshape(n_grp, n_mem, rhs, per), (2, 1, 0, 3))
        return pieces_all.reshape(rhs, B)

    def to_block(gathered, rows):
        return jnp.transpose(gathered, (1, 0, 2)).reshape(rows, B)

    block0, block1 = order[0], order[1]
    sel0 = selector(block0)
    sel1 = selector(block1)
    plain = (((1,), (0,)), ((), ()))
    chosen = exact_dot(
        jnp.concatenate([residual, points], axis=0), jnp.concatenate([sel0, sel1], axis=1), plain
    )
    chosen0 = chosen[:, :per]
    res1_start = chosen[:rhs, per:]
    pts1_local = chosen[rhs:, per:]
    gathered = to_block(gather_all(jnp.concatenate([chosen0, pts1_local], axis=0), n_dev), rhs + 2 * feat)
    block_res0 = gathered[:rhs]
    block_pts0 = gathered[rhs:rhs + feat]
    block_pts1 = gathered[rhs + feat:]

    delta0 = solve(block_res0, block0)
    owned0 = lax.dynamic_slice_in_dim(delta0, mine * per, per, axis=1)
    kernel0 = kern(points, block_pts0)
    early = apply_kernel(delta0, kern(pts1_local, block_pts0))
    overlap = lax.dot_general(sel0, sel1, (((0,), (0,)), ((), ())), preferred_element_type=jnp.float32)
    overlap = overlap.astype(jnp.bfloat16)
    res1_local = res1_start - early - ridge_weight * exact_dot(owned0, overlap, plain)
    res1_local, pts_late, pts1_late = lax.optimization_barrier((res1_local, points, block_pts1))
    block_res1 = to_block(gather_all(res1_local, n_dev), rhs)
    kernel1 = kern(pts_late, pts1_late)

    solved1 = solve_rows(inverse, block1 % slots, block_res1)
    solved1, delta0_late = lax.optimization_barrier((solved1, delta0))
    delta1 = distribute(solved1, block1)
    spread0 = exact_dot(owned0, sel0, (((1,), (1,)), ((), ())))
    update0 = apply_kernel(delta0_late, kernel0)
    residual = residual - update0 - ridge_weight * spread0
    coef = coef + spread0

    owned1 = lax.dynamic_slice_in_dim(delta1, mine * per, per, axis=1)
    spread1 = exact_dot(owned1, sel1, (((1,), (1,)), ((), ())))
    update1 = apply_kernel(delta1, kernel1)
    residual = residual - update1 - ridge_weight * spread1
    coef = coef + spread1
    return (residual, coef)


def solution(mesh):
    in_specs = (
        P(None, ("grp", "mem")),
        P(None, ("grp", "mem")),
        P(None, ("grp", "mem")),
        P(("grp", "mem")),
        P(),
        P("grp", "mem", None),
    )
    out_specs = (P(None, ("grp", "mem")), P(None, ("grp", "mem")))
    return jax.shard_map(body, mesh=mesh, in_specs=in_specs, out_specs=out_specs, check_vma=False)
```

```python
import jax
import jax.numpy as jnp
from jax import lax
from jax.sharding import PartitionSpec as P
from jax.experimental import pallas as pl
from jax.experimental.pallas import tpu as pltpu

B = 4096
STEPS = 2

ridge_weight = 0.5
kernel_scale = 0.125
ALL = ("grp", "mem")
HIGHEST = lax.Precision.HIGHEST
HIGH = lax.Precision.HIGH


def gather_all(piece, n_dev):
    sent = jnp.broadcast_to(piece[None], (n_dev,) + piece.shape)
    return lax.all_to_all(sent, ALL, 0, 0, tiled=True)


def split3(x):
    x1 = lax.reduce_precision(x, exponent_bits=8, mantissa_bits=7)
    r1 = x - x1
    x2 = lax.reduce_precision(r1, exponent_bits=8, mantissa_bits=7)
    r2 = r1 - x2
    return x1.astype(jnp.bfloat16), x2.astype(jnp.bfloat16), r2.astype(jnp.bfloat16)


def kern(u, v):
    nu = jnp.sum(u * u, axis=0)
    nv = jnp.sum(v * v, axis=0)
    u1, u2, u3 = split3(u)
    v1, v2, v3 = split3(-2.0 * v)
    left = jnp.concatenate([u1, u1, u2, u1, u3, u2], axis=0)
    right = jnp.concatenate([v1, v2, v1, v3, v1, v2], axis=0)
    cross2 = lax.dot_general(left, right, (((0,), (0,)), ((), ())), preferred_element_type=jnp.float32)
    kernel = jnp.exp(-kernel_scale * ((nu[:, None] + nv[None, :]) + cross2))
    k1 = lax.reduce_precision(kernel, exponent_bits=8, mantissa_bits=7)
    return lax.optimization_barrier((k1.astype(jnp.bfloat16), (kernel - k1).astype(jnp.bfloat16)))


def apply_kernel(delta, kernel):
    k1, k2 = kernel
    d1f = lax.reduce_precision(delta, exponent_bits=8, mantissa_bits=7)
    d1 = d1f.astype(jnp.bfloat16)
    d2 = (delta - d1f).astype(jnp.bfloat16)
    rows = delta.shape[0]
    dims = (((1,), (1,)), ((), ()))
    both = lax.dot_general(jnp.concatenate([d1, d2], axis=0), k1, dims, preferred_element_type=jnp.float32)
    low = lax.dot_general(d1, k2, dims, preferred_element_type=jnp.float32)
    return (both[:rows] + both[rows:]) + low


def exact_dot(x, onehot, dims):
    rows = x.shape[0]
    parts = jnp.concatenate(split3(x), axis=0)
    out = lax.dot_general(parts, onehot, dims, preferred_element_type=jnp.float32)
    return (out[:rows] + out[rows:2 * rows]) + out[2 * rows:]


def solve_kernel(slot_ref, inv_ref, rcat_ref, r1_ref, o_ref):
    a = inv_ref[...]
    hi = a.astype(jnp.bfloat16)
    lo = (a - hi.astype(jnp.float32)).astype(jnp.bfloat16)
    dims = (((1,), (1,)), ((), ()))
    both = lax.dot_general(rcat_ref[...], hi, dims, preferred_element_type=jnp.float32)
    low = lax.dot_general(r1_ref[...], lo, dims, preferred_element_type=jnp.float32)
    rows = o_ref.shape[0]
    o_ref[...] = (both[:rows] + both[rows:]) + low


def solve_rows(inverse, slot, block_res, tile=512):
    _, n, width = inverse.shape
    rows = block_res.shape[0]
    r1f = lax.reduce_precision(block_res, exponent_bits=8, mantissa_bits=7)
    r1 = r1f.astype(jnp.bfloat16)
    r2 = (block_res - r1f).astype(jnp.bfloat16)
    rcat = jnp.concatenate([r1, r2], axis=0)
    tile = min(tile, n)
    grid_spec = pltpu.PrefetchScalarGridSpec(
        num_scalar_prefetch=1,
        grid=(n // tile,),
        in_specs=[
            pl.BlockSpec((None, tile, width), lambda i, s: (s[0], i, 0)),
            pl.BlockSpec((2 * rows, width), lambda i, s: (0, 0)),
            pl.BlockSpec((rows, width), lambda i, s: (0, 0)),
        ],
        out_specs=pl.BlockSpec((rows, tile), lambda i, s: (0, i)),
    )
    return pl.pallas_call(
        solve_kernel,
        grid_spec=grid_spec,
        out_shape=jax.ShapeDtypeStruct((rows, n), jnp.float32),
        compiler_params=pltpu.CompilerParams(vmem_limit_bytes=48 * 1024 * 1024),
        cost_estimate=pl.CostEstimate(
            flops=6 * rows * n * width, transcendentals=0, bytes_accessed=4 * n * width
        ),
    )(jnp.reshape(slot, (1,)).astype(jnp.int32), inverse, rcat, r1)


def body(points, residual, coef, block_of, order, inverse):
    n_grp = lax.axis_size("grp")
    n_mem = lax.axis_size("mem")
    n_dev = n_grp * n_mem
    per = B // n_dev
    slots = inverse.shape[0]
    feat = points.shape[0]
    rhs = residual.shape[0]
    mine = lax.axis_index("grp") * n_mem + lax.axis_index("mem")

    def selector(block_id):
        inside = block_of == block_id
        position = jnp.cumsum(inside.astype(jnp.int32)) - 1
        return (
            (position[:, None] == jnp.arange(per, dtype=jnp.int32)[None, :]) & inside[:, None]
        ).astype(jnp.bfloat16)

    def solve(block_res, block_id):
        return distribute(solve_rows(inverse, block_id % slots, block_res), block_id)

    def distribute(solved, block_id):
        owner = block_id // slots
        pieces = jnp.transpose(solved.reshape(rhs, n_grp, per), (1, 0, 2))
        scattered = lax.all_to_all(pieces, "grp", 0, 0, tiled=True)
        piece = lax.dynamic_index_in_dim(scattered, owner, 0, keepdims=False)
        pieces_all = gather_all(piece, n_dev)
        pieces_all = jnp.transpose(pieces_all.reshape(n_grp, n_mem, rhs, per), (2, 1, 0, 3))
        return pieces_all.reshape(rhs, B)

    def to_block(gathered, rows):
        return jnp.transpose(gathered, (1, 0, 2)).reshape(rows, B)

    block0, block1 = order[0], order[1]
    sel0 = selector(block0)
    sel1 = selector(block1)
    plain = (((1,), (0,)), ((), ()))
    chosen = exact_dot(
        jnp.concatenate([residual, points], axis=0), jnp.concatenate([sel0, sel1], axis=1), plain
    )
    chosen0 = chosen[:, :per]
    res1_start = chosen[:rhs, per:]
    pts1_local = chosen[rhs:, per:]
    gathered = to_block(gather_all(jnp.concatenate([chosen0, pts1_local], axis=0), n_dev), rhs + 2 * feat)
    block_res0 = gathered[:rhs]
    block_pts0 = gathered[rhs:rhs + feat]
    block_pts1 = gathered[rhs + feat:]

    delta0 = solve(block_res0, block0)
    owned0 = lax.dynamic_slice_in_dim(delta0, mine * per, per, axis=1)
    kernel0 = kern(points, block_pts0)
    early = apply_kernel(delta0, kern(pts1_local, block_pts0))
    overlap = lax.dot_general(sel0, sel1, (((0,), (0,)), ((), ())), preferred_element_type=jnp.float32)
    overlap = overlap.astype(jnp.bfloat16)
    res1_local = res1_start - early - ridge_weight * exact_dot(owned0, overlap, plain)
    res1_local, pts_late, pts1_late = lax.optimization_barrier((res1_local, points, block_pts1))
    block_res1 = to_block(gather_all(res1_local, n_dev), rhs)
    kernel1 = kern(pts_late, pts1_late)

    solved1 = solve_rows(inverse, block1 % slots, block_res1)
    solved1, delta0_late = lax.optimization_barrier((solved1, delta0))
    delta1 = distribute(solved1, block1)
    spread0 = exact_dot(owned0, sel0, (((1,), (1,)), ((), ())))
    update0 = apply_kernel(delta0_late, kernel0)
    residual = residual - update0 - ridge_weight * spread0
    coef = coef + spread0

    owned1 = lax.dynamic_slice_in_dim(delta1, mine * per, per, axis=1)
    spread1 = exact_dot(owned1, sel1, (((1,), (1,)), ((), ())))
    update1 = apply_kernel(delta1, kernel1)
    residual = residual - update1 - ridge_weight * spread1
    coef = coef + spread1
    return (residual, coef)


def solution(mesh):
    in_specs = (
        P(None, ("grp", "mem")),
        P(None, ("grp", "mem")),
        P(None, ("grp", "mem")),
        P(("grp", "mem")),
        P(),
        P("grp", "mem", None),
    )
    out_specs = (P(None, ("grp", "mem")), P(None, ("grp", "mem")))
    return jax.shard_map(body, mesh=mesh, in_specs=in_specs, out_specs=out_specs, check_vma=False)
```

```python
import jax
import jax.numpy as jnp
from jax import lax
from jax.sharding import PartitionSpec as P
from jax.experimental import pallas as pl
from jax.experimental.pallas import tpu as pltpu

B = 4096
STEPS = 2

ridge_weight = 0.5
kernel_scale = 0.125
ALL = ("grp", "mem")
HIGHEST = lax.Precision.HIGHEST
HIGH = lax.Precision.HIGH


def gather_all(piece, n_dev):
    sent = jnp.broadcast_to(piece[None], (n_dev,) + piece.shape)
    return lax.all_to_all(sent, ALL, 0, 0, tiled=True)


def split3(x):
    x1 = lax.reduce_precision(x, exponent_bits=8, mantissa_bits=7)
    r1 = x - x1
    x2 = lax.reduce_precision(r1, exponent_bits=8, mantissa_bits=7)
    r2 = r1 - x2
    return x1.astype(jnp.bfloat16), x2.astype(jnp.bfloat16), r2.astype(jnp.bfloat16)


def kern(u, v):
    nu = jnp.sum(u * u, axis=0)
    nv = jnp.sum(v * v, axis=0)
    u1, u2, u3 = split3(u)
    v1, v2, v3 = split3(-2.0 * v)
    left = jnp.concatenate([u1, u1, u2, u1, u3, u2], axis=0)
    right = jnp.concatenate([v1, v2, v1, v3, v1, v2], axis=0)
    cross2 = lax.dot_general(left, right, (((0,), (0,)), ((), ())), preferred_element_type=jnp.float32)
    kernel = jnp.exp(-kernel_scale * ((nu[:, None] + nv[None, :]) + cross2))
    return lax.optimization_barrier(kernel)


def apply_kernel(delta, kernel):
    return lax.dot_general(delta, kernel, (((1,), (1,)), ((), ())), precision=HIGH)


def exact_dot(x, onehot, dims):
    rows = x.shape[0]
    parts = jnp.concatenate(split3(x), axis=0)
    out = lax.dot_general(parts, onehot, dims, preferred_element_type=jnp.float32)
    return (out[:rows] + out[rows:2 * rows]) + out[2 * rows:]


def solve_kernel(slot_ref, inv_ref, rcat_ref, r1_ref, o_ref):
    a = inv_ref[...]
    hi = a.astype(jnp.bfloat16)
    lo = (a - hi.astype(jnp.float32)).astype(jnp.bfloat16)
    dims = (((1,), (1,)), ((), ()))
    both = lax.dot_general(rcat_ref[...], hi, dims, preferred_element_type=jnp.float32)
    low = lax.dot_general(r1_ref[...], lo, dims, preferred_element_type=jnp.float32)
    rows = o_ref.shape[0]
    o_ref[...] = (both[:rows] + both[rows:]) + low


def solve_rows(inverse, slot, block_res, tile=512):
    _, n, width = inverse.shape
    rows = block_res.shape[0]
    r1f = lax.reduce_precision(block_res, exponent_bits=8, mantissa_bits=7)
    r1 = r1f.astype(jnp.bfloat16)
    r2 = (block_res - r1f).astype(jnp.bfloat16)
    rcat = jnp.concatenate([r1, r2], axis=0)
    tile = min(tile, n)
    grid_spec = pltpu.PrefetchScalarGridSpec(
        num_scalar_prefetch=1,
        grid=(n // tile,),
        in_specs=[
            pl.BlockSpec((None, tile, width), lambda i, s: (s[0], i, 0)),
            pl.BlockSpec((2 * rows, width), lambda i, s: (0, 0)),
            pl.BlockSpec((rows, width), lambda i, s: (0, 0)),
        ],
        out_specs=pl.BlockSpec((rows, tile), lambda i, s: (0, i)),
    )
    return pl.pallas_call(
        solve_kernel,
        grid_spec=grid_spec,
        out_shape=jax.ShapeDtypeStruct((rows, n), jnp.float32),
        compiler_params=pltpu.CompilerParams(vmem_limit_bytes=48 * 1024 * 1024),
        cost_estimate=pl.CostEstimate(
            flops=6 * rows * n * width, transcendentals=0, bytes_accessed=4 * n * width
        ),
    )(jnp.reshape(slot, (1,)).astype(jnp.int32), inverse, rcat, r1)


def body(points, residual, coef, block_of, order, inverse):
    n_grp = lax.axis_size("grp")
    n_mem = lax.axis_size("mem")
    n_dev = n_grp * n_mem
    per = B // n_dev
    slots = inverse.shape[0]
    feat = points.shape[0]
    rhs = residual.shape[0]
    mine = lax.axis_index("grp") * n_mem + lax.axis_index("mem")

    def selector(block_id):
        inside = block_of == block_id
        position = jnp.cumsum(inside.astype(jnp.int32)) - 1
        return (
            (position[:, None] == jnp.arange(per, dtype=jnp.int32)[None, :]) & inside[:, None]
        ).astype(jnp.bfloat16)

    def solve(block_res, block_id):
        return distribute(solve_rows(inverse, block_id % slots, block_res), block_id)

    def distribute(solved, block_id):
        owner = block_id // slots
        pieces = jnp.transpose(solved.reshape(rhs, n_grp, per), (1, 0, 2))
        scattered = lax.all_to_all(pieces, "grp", 0, 0, tiled=True)
        piece = lax.dynamic_index_in_dim(scattered, owner, 0, keepdims=False)
        pieces_all = gather_all(piece, n_dev)
        pieces_all = jnp.transpose(pieces_all.reshape(n_grp, n_mem, rhs, per), (2, 1, 0, 3))
        return pieces_all.reshape(rhs, B)

    def to_block(gathered, rows):
        return jnp.transpose(gathered, (1, 0, 2)).reshape(rows, B)

    block0, block1 = order[0], order[1]
    sel0 = selector(block0)
    sel1 = selector(block1)
    plain = (((1,), (0,)), ((), ()))
    chosen = exact_dot(
        jnp.concatenate([residual, points], axis=0), jnp.concatenate([sel0, sel1], axis=1), plain
    )
    chosen0 = chosen[:, :per]
    res1_start = chosen[:rhs, per:]
    pts1_local = chosen[rhs:, per:]
    gathered = to_block(gather_all(jnp.concatenate([chosen0, pts1_local], axis=0), n_dev), rhs + 2 * feat)
    block_res0 = gathered[:rhs]
    block_pts0 = gathered[rhs:rhs + feat]
    block_pts1 = gathered[rhs + feat:]

    delta0 = solve(block_res0, block0)
    owned0 = lax.dynamic_slice_in_dim(delta0, mine * per, per, axis=1)
    kernel0 = kern(points, block_pts0)
    early = apply_kernel(delta0, kern(pts1_local, block_pts0))
    overlap = lax.dot_general(sel0, sel1, (((0,), (0,)), ((), ())), preferred_element_type=jnp.float32)
    overlap = overlap.astype(jnp.bfloat16)
    res1_local = res1_start - early - ridge_weight * exact_dot(owned0, overlap, plain)
    res1_local, pts_late, pts1_late = lax.optimization_barrier((res1_local, points, block_pts1))
    block_res1 = to_block(gather_all(res1_local, n_dev), rhs)
    kernel1 = kern(pts_late, pts1_late)

    solved1 = solve_rows(inverse, block1 % slots, block_res1)
    solved1, delta0_late = lax.optimization_barrier((solved1, delta0))
    delta1 = distribute(solved1, block1)
    spread0 = exact_dot(owned0, sel0, (((1,), (1,)), ((), ())))
    update0 = apply_kernel(delta0_late, kernel0)
    residual = residual - update0 - ridge_weight * spread0
    coef = coef + spread0

    owned1 = lax.dynamic_slice_in_dim(delta1, mine * per, per, axis=1)
    spread1 = exact_dot(owned1, sel1, (((1,), (1,)), ((), ())))
    update1 = apply_kernel(delta1, kernel1)
    residual = residual - update1 - ridge_weight * spread1
    coef = coef + spread1
    return (residual, coef)


def solution(mesh):
    in_specs = (
        P(None, ("grp", "mem")),
        P(None, ("grp", "mem")),
        P(None, ("grp", "mem")),
        P(("grp", "mem")),
        P(),
        P("grp", "mem", None),
    )
    out_specs = (P(None, ("grp", "mem")), P(None, ("grp", "mem")))
    return jax.shard_map(body, mesh=mesh, in_specs=in_specs, out_specs=out_specs, check_vma=False)
```

```python
import jax
import jax.numpy as jnp
from jax import lax
from jax.sharding import PartitionSpec as P
from jax.experimental import pallas as pl
from jax.experimental.pallas import tpu as pltpu

B = 4096
STEPS = 2

ridge_weight = 0.5
kernel_scale = 0.125
ALL = ("grp", "mem")
HIGHEST = lax.Precision.HIGHEST
HIGH = lax.Precision.HIGH


def gather_all(piece, n_dev):
    sent = jnp.broadcast_to(piece[None], (n_dev,) + piece.shape)
    return lax.all_to_all(sent, ALL, 0, 0, tiled=True)


def split3(x):
    x1 = lax.reduce_precision(x, exponent_bits=8, mantissa_bits=7)
    r1 = x - x1
    x2 = lax.reduce_precision(r1, exponent_bits=8, mantissa_bits=7)
    r2 = r1 - x2
    return x1.astype(jnp.bfloat16), x2.astype(jnp.bfloat16), r2.astype(jnp.bfloat16)


def kern(u, v):
    nu = jnp.sum(u * u, axis=0)
    nv = jnp.sum(v * v, axis=0)
    u1, u2, u3 = split3(u)
    v1, v2, v3 = split3(-2.0 * v)
    left = jnp.concatenate([u1, u1, u2, u1, u3, u2], axis=0)
    right = jnp.concatenate([v1, v2, v1, v3, v1, v2], axis=0)
    cross2 = lax.dot_general(left, right, (((0,), (0,)), ((), ())), preferred_element_type=jnp.float32)
    kernel = jnp.exp(-kernel_scale * ((nu[:, None] + nv[None, :]) + cross2))
    return lax.optimization_barrier(kernel)


def apply_kernel(delta, kernel):
    return lax.dot_general(delta, kernel, (((1,), (1,)), ((), ())), precision=HIGH)


def exact_dot(x, onehot, dims):
    rows = x.shape[0]
    parts = jnp.concatenate(split3(x), axis=0)
    out = lax.dot_general(parts, onehot, dims, preferred_element_type=jnp.float32)
    return (out[:rows] + out[rows:2 * rows]) + out[2 * rows:]


def solve_kernel(slot_ref, inv_ref, rcat_ref, r1_ref, o_ref):
    a = inv_ref[...]
    hi = a.astype(jnp.bfloat16)
    lo = (a - hi.astype(jnp.float32)).astype(jnp.bfloat16)
    dims = (((1,), (1,)), ((), ()))
    both = lax.dot_general(rcat_ref[...], hi, dims, preferred_element_type=jnp.float32)
    low = lax.dot_general(r1_ref[...], lo, dims, preferred_element_type=jnp.float32)
    rows = o_ref.shape[0]
    o_ref[...] = (both[:rows] + both[rows:]) + low


def solve_rows(inverse, slot, block_res, tile=512):
    _, n, width = inverse.shape
    rows = block_res.shape[0]
    r1f = lax.reduce_precision(block_res, exponent_bits=8, mantissa_bits=7)
    r1 = r1f.astype(jnp.bfloat16)
    r2 = (block_res - r1f).astype(jnp.bfloat16)
    rcat = jnp.concatenate([r1, r2], axis=0)
    tile = min(tile, n)
    grid_spec = pltpu.PrefetchScalarGridSpec(
        num_scalar_prefetch=1,
        grid=(n // tile,),
        in_specs=[
            pl.BlockSpec((None, tile, width), lambda i, s: (s[0], i, 0)),
            pl.BlockSpec((2 * rows, width), lambda i, s: (0, 0)),
            pl.BlockSpec((rows, width), lambda i, s: (0, 0)),
        ],
        out_specs=pl.BlockSpec((rows, tile), lambda i, s: (0, i)),
    )
    return pl.pallas_call(
        solve_kernel,
        grid_spec=grid_spec,
        out_shape=jax.ShapeDtypeStruct((rows, n), jnp.float32),
        compiler_params=pltpu.CompilerParams(vmem_limit_bytes=48 * 1024 * 1024),
        cost_estimate=pl.CostEstimate(
            flops=6 * rows * n * width, transcendentals=0, bytes_accessed=4 * n * width
        ),
    )(jnp.reshape(slot, (1,)).astype(jnp.int32), inverse, rcat, r1)


def body(points, residual, coef, block_of, order, inverse):
    n_grp = lax.axis_size("grp")
    n_mem = lax.axis_size("mem")
    n_dev = n_grp * n_mem
    per = B // n_dev
    slots = inverse.shape[0]
    feat = points.shape[0]
    rhs = residual.shape[0]
    mine = lax.axis_index("grp") * n_mem + lax.axis_index("mem")

    def selector(block_id):
        inside = block_of == block_id
        position = jnp.cumsum(inside.astype(jnp.int32)) - 1
        return (
            (position[:, None] == jnp.arange(per, dtype=jnp.int32)[None, :]) & inside[:, None]
        ).astype(jnp.bfloat16)

    def solve(block_res, block_id):
        return distribute(solve_rows(inverse, block_id % slots, block_res), block_id)

    def distribute(solved, block_id):
        owner = block_id // slots
        pieces = jnp.transpose(solved.reshape(rhs, n_grp, per), (1, 0, 2))
        scattered = lax.all_to_all(pieces, "grp", 0, 0, tiled=True)
        piece = lax.dynamic_index_in_dim(scattered, owner, 0, keepdims=False)
        pieces_all = gather_all(piece, n_dev)
        pieces_all = jnp.transpose(pieces_all.reshape(n_grp, n_mem, rhs, per), (2, 1, 0, 3))
        return pieces_all.reshape(rhs, B)

    def to_block(gathered, rows):
        return jnp.transpose(gathered, (1, 0, 2)).reshape(rows, B)

    block0, block1 = order[0], order[1]
    sel0 = selector(block0)
    sel1 = selector(block1)
    plain = (((1,), (0,)), ((), ()))
    chosen = exact_dot(
        jnp.concatenate([residual, points], axis=0), jnp.concatenate([sel0, sel1], axis=1), plain
    )
    chosen0 = chosen[:, :per]
    res1_start = chosen[:rhs, per:]
    pts1_local = chosen[rhs:, per:]
    gathered = to_block(gather_all(jnp.concatenate([chosen0, pts1_local], axis=0), n_dev), rhs + 2 * feat)
    block_res0 = gathered[:rhs]
    block_pts0 = gathered[rhs:rhs + feat]
    block_pts1 = gathered[rhs + feat:]

    delta0 = solve(block_res0, block0)
    owned0 = lax.dynamic_slice_in_dim(delta0, mine * per, per, axis=1)
    kernel0 = kern(points, block_pts0)
    early = apply_kernel(delta0, kern(pts1_local, block_pts0))
    overlap = lax.dot_general(sel0, sel1, (((0,), (0,)), ((), ())), preferred_element_type=jnp.float32)
    overlap = overlap.astype(jnp.bfloat16)
    res1_local = res1_start - early - ridge_weight * exact_dot(owned0, overlap, plain)
    res1_local, pts_late, pts1_late = lax.optimization_barrier((res1_local, points, block_pts1))
    block_res1 = to_block(gather_all(res1_local, n_dev), rhs)
    kernel1 = kern(pts_late, pts1_late)

    solved1 = solve_rows(inverse, block1 % slots, block_res1)
    solved1, delta0_late = lax.optimization_barrier((solved1, delta0))
    delta1 = distribute(solved1, block1)
    spread0 = exact_dot(owned0, sel0, (((1,), (1,)), ((), ())))
    half = kernel0.shape[0] // 2
    update0 = jnp.concatenate(
        [apply_kernel(delta0_late, kernel0[:half]), apply_kernel(delta0_late, kernel0[half:])], axis=1
    )
    residual = residual - update0 - ridge_weight * spread0
    coef = coef + spread0

    owned1 = lax.dynamic_slice_in_dim(delta1, mine * per, per, axis=1)
    spread1 = exact_dot(owned1, sel1, (((1,), (1,)), ((), ())))
    update1 = apply_kernel(delta1, kernel1)
    residual = residual - update1 - ridge_weight * spread1
    coef = coef + spread1
    return (residual, coef)


def solution(mesh):
    in_specs = (
        P(None, ("grp", "mem")),
        P(None, ("grp", "mem")),
        P(None, ("grp", "mem")),
        P(("grp", "mem")),
        P(),
        P("grp", "mem", None),
    )
    out_specs = (P(None, ("grp", "mem")), P(None, ("grp", "mem")))
    return jax.shard_map(body, mesh=mesh, in_specs=in_specs, out_specs=out_specs, check_vma=False)
```

```python
import jax
import jax.numpy as jnp
from jax import lax
from jax.sharding import PartitionSpec as P
from jax.experimental import pallas as pl
from jax.experimental.pallas import tpu as pltpu

B = 4096
STEPS = 2

ridge_weight = 0.5
kernel_scale = 0.125
ALL = ("grp", "mem")
HIGHEST = lax.Precision.HIGHEST
HIGH = lax.Precision.HIGH


def gather_all(piece, n_dev):
    sent = jnp.broadcast_to(piece[None], (n_dev,) + piece.shape)
    return lax.all_to_all(sent, ALL, 0, 0, tiled=True)


def split3(x):
    x1 = lax.reduce_precision(x, exponent_bits=8, mantissa_bits=7)
    r1 = x - x1
    x2 = lax.reduce_precision(r1, exponent_bits=8, mantissa_bits=7)
    r2 = r1 - x2
    return x1.astype(jnp.bfloat16), x2.astype(jnp.bfloat16), r2.astype(jnp.bfloat16)


def kern(u, v):
    nu = jnp.sum(u * u, axis=0)
    nv = jnp.sum(v * v, axis=0)
    u1, u2, u3 = split3(u)
    v1, v2, v3 = split3(-2.0 * v)
    left = jnp.concatenate([u1, u1, u2, u1, u3, u2], axis=0)
    right = jnp.concatenate([v1, v2, v1, v3, v1, v2], axis=0)
    cross2 = lax.dot_general(left, right, (((0,), (0,)), ((), ())), preferred_element_type=jnp.float32)
    kernel = jnp.exp(-kernel_scale * ((nu[:, None] + nv[None, :]) + cross2))
    return lax.optimization_barrier(kernel)


def apply_kernel(delta, kernel):
    return lax.dot_general(delta, kernel, (((1,), (1,)), ((), ())), precision=HIGH)


def exact_dot(x, onehot, dims):
    rows = x.shape[0]
    parts = jnp.concatenate(split3(x), axis=0)
    out = lax.dot_general(parts, onehot, dims, preferred_element_type=jnp.float32)
    return (out[:rows] + out[rows:2 * rows]) + out[2 * rows:]


def solve_kernel(slot_ref, inv_ref, rcat_ref, r1_ref, o_ref):
    a = inv_ref[...]
    hi = a.astype(jnp.bfloat16)
    lo = (a - hi.astype(jnp.float32)).astype(jnp.bfloat16)
    dims = (((1,), (1,)), ((), ()))
    both = lax.dot_general(hi, rcat_ref[...], dims, preferred_element_type=jnp.float32)
    low = lax.dot_general(lo, r1_ref[...], dims, preferred_element_type=jnp.float32)
    rows = o_ref.shape[1]
    o_ref[...] = (both[:, :rows] + both[:, rows:]) + low


def solve_rows(inverse, slot, block_res, tile=512):
    _, n, width = inverse.shape
    rows = block_res.shape[0]
    r1f = lax.reduce_precision(block_res, exponent_bits=8, mantissa_bits=7)
    r1 = r1f.astype(jnp.bfloat16)
    r2 = (block_res - r1f).astype(jnp.bfloat16)
    rcat = jnp.concatenate([r1, r2], axis=0)
    tile = min(tile, n)
    grid_spec = pltpu.PrefetchScalarGridSpec(
        num_scalar_prefetch=1,
        grid=(n // tile,),
        in_specs=[
            pl.BlockSpec((None, tile, width), lambda i, s: (s[0], i, 0)),
            pl.BlockSpec((2 * rows, width), lambda i, s: (0, 0)),
            pl.BlockSpec((rows, width), lambda i, s: (0, 0)),
        ],
        out_specs=pl.BlockSpec((tile, rows), lambda i, s: (i, 0)),
    )
    return pl.pallas_call(
        solve_kernel,
        grid_spec=grid_spec,
        out_shape=jax.ShapeDtypeStruct((n, rows), jnp.float32),
        compiler_params=pltpu.CompilerParams(vmem_limit_bytes=48 * 1024 * 1024),
        cost_estimate=pl.CostEstimate(
            flops=6 * rows * n * width, transcendentals=0, bytes_accessed=4 * n * width
        ),
    )(jnp.reshape(slot, (1,)).astype(jnp.int32), inverse, rcat, r1).T


def body(points, residual, coef, block_of, order, inverse):
    n_grp = lax.axis_size("grp")
    n_mem = lax.axis_size("mem")
    n_dev = n_grp * n_mem
    per = B // n_dev
    slots = inverse.shape[0]
    feat = points.shape[0]
    rhs = residual.shape[0]
    mine = lax.axis_index("grp") * n_mem + lax.axis_index("mem")

    def selector(block_id):
        inside = block_of == block_id
        position = jnp.cumsum(inside.astype(jnp.int32)) - 1
        return (
            (position[:, None] == jnp.arange(per, dtype=jnp.int32)[None, :]) & inside[:, None]
        ).astype(jnp.bfloat16)

    def solve(block_res, block_id):
        return distribute(solve_rows(inverse, block_id % slots, block_res), block_id)

    def distribute(solved, block_id):
        owner = block_id // slots
        pieces = jnp.transpose(solved.reshape(rhs, n_grp, per), (1, 0, 2))
        scattered = lax.all_to_all(pieces, "grp", 0, 0, tiled=True)
        piece = lax.dynamic_index_in_dim(scattered, owner, 0, keepdims=False)
        pieces_all = gather_all(piece, n_dev)
        pieces_all = jnp.transpose(pieces_all.reshape(n_grp, n_mem, rhs, per), (2, 1, 0, 3))
        return pieces_all.reshape(rhs, B)

    def to_block(gathered, rows):
        return jnp.transpose(gathered, (1, 0, 2)).reshape(rows, B)

    block0, block1 = order[0], order[1]
    sel0 = selector(block0)
    sel1 = selector(block1)
    plain = (((1,), (0,)), ((), ()))
    chosen = exact_dot(
        jnp.concatenate([residual, points], axis=0), jnp.concatenate([sel0, sel1], axis=1), plain
    )
    chosen0 = chosen[:, :per]
    res1_start = chosen[:rhs, per:]
    pts1_local = chosen[rhs:, per:]
    gathered = to_block(gather_all(jnp.concatenate([chosen0, pts1_local], axis=0), n_dev), rhs + 2 * feat)
    block_res0 = gathered[:rhs]
    block_pts0 = gathered[rhs:rhs + feat]
    block_pts1 = gathered[rhs + feat:]

    delta0 = solve(block_res0, block0)
    owned0 = lax.dynamic_slice_in_dim(delta0, mine * per, per, axis=1)
    kernel0 = kern(points, block_pts0)
    early = apply_kernel(delta0, kern(pts1_local, block_pts0))
    overlap = lax.dot_general(sel0, sel1, (((0,), (0,)), ((), ())), preferred_element_type=jnp.float32)
    overlap = overlap.astype(jnp.bfloat16)
    res1_local = res1_start - early - ridge_weight * exact_dot(owned0, overlap, plain)
    res1_local, pts_late, pts1_late = lax.optimization_barrier((res1_local, points, block_pts1))
    block_res1 = to_block(gather_all(res1_local, n_dev), rhs)
    kernel1 = kern(pts_late, pts1_late)

    solved1 = solve_rows(inverse, block1 % slots, block_res1)
    solved1, delta0_late = lax.optimization_barrier((solved1, delta0))
    delta1 = distribute(solved1, block1)
    spread0 = exact_dot(owned0, sel0, (((1,), (1,)), ((), ())))
    update0 = apply_kernel(delta0_late, kernel0)
    residual = residual - update0 - ridge_weight * spread0
    coef = coef + spread0

    owned1 = lax.dynamic_slice_in_dim(delta1, mine * per, per, axis=1)
    spread1 = exact_dot(owned1, sel1, (((1,), (1,)), ((), ())))
    update1 = apply_kernel(delta1, kernel1)
    residual = residual - update1 - ridge_weight * spread1
    coef = coef + spread1
    return (residual, coef)


def solution(mesh):
    in_specs = (
        P(None, ("grp", "mem")),
        P(None, ("grp", "mem")),
        P(None, ("grp", "mem")),
        P(("grp", "mem")),
        P(),
        P("grp", "mem", None),
    )
    out_specs = (P(None, ("grp", "mem")), P(None, ("grp", "mem")))
    return jax.shard_map(body, mesh=mesh, in_specs=in_specs, out_specs=out_specs, check_vma=False)
```

```python
import jax
import jax.numpy as jnp
from jax import lax
from jax.sharding import PartitionSpec as P
from jax.experimental import pallas as pl
from jax.experimental.pallas import tpu as pltpu

B = 4096
STEPS = 2

ridge_weight = 0.5
kernel_scale = 0.125
ALL = ("grp", "mem")
HIGHEST = lax.Precision.HIGHEST
HIGH = lax.Precision.HIGH


def gather_all(piece, n_dev):
    sent = jnp.broadcast_to(piece[None], (n_dev,) + piece.shape)
    return lax.all_to_all(sent, ALL, 0, 0, tiled=True)


def split3(x):
    x1 = lax.reduce_precision(x, exponent_bits=8, mantissa_bits=7)
    r1 = x - x1
    x2 = lax.reduce_precision(r1, exponent_bits=8, mantissa_bits=7)
    r2 = r1 - x2
    return x1.astype(jnp.bfloat16), x2.astype(jnp.bfloat16), r2.astype(jnp.bfloat16)


def kern(u, v):
    nu = jnp.sum(u * u, axis=0)
    nv = jnp.sum(v * v, axis=0)
    u1, u2, u3 = split3(u)
    v1, v2, v3 = split3(-2.0 * v)
    left = jnp.concatenate([u1, u1, u2, u1, u3, u2], axis=0)
    right = jnp.concatenate([v1, v2, v1, v3, v1, v2], axis=0)
    cross2 = lax.dot_general(left, right, (((0,), (0,)), ((), ())), preferred_element_type=jnp.float32)
    kernel = jnp.exp(-kernel_scale * ((nu[:, None] + nv[None, :]) + cross2))
    k1 = lax.reduce_precision(kernel, exponent_bits=8, mantissa_bits=7)
    return lax.optimization_barrier((k1.astype(jnp.bfloat16), (kernel - k1).astype(jnp.bfloat16)))


def product_kernel(k1_ref, k2_ref, d12_ref, d1_ref, o_ref):
    dims = (((1,), (1,)), ((), ()))
    both = lax.dot_general(k1_ref[...], d12_ref[...], dims, preferred_element_type=jnp.float32)
    low = lax.dot_general(k2_ref[...], d1_ref[...], dims, preferred_element_type=jnp.float32)
    rows = o_ref.shape[1]
    o_ref[...] = (both[:, :rows] + both[:, rows:]) + low


def apply_kernel(delta, kernel, tile=256):
    k1, k2 = kernel
    n, m = k1.shape
    rows = delta.shape[0]
    d1f = lax.reduce_precision(delta, exponent_bits=8, mantissa_bits=7)
    d1 = d1f.astype(jnp.bfloat16)
    d2 = (delta - d1f).astype(jnp.bfloat16)
    d12 = jnp.concatenate([d1, d2], axis=0)
    tile = min(tile, n)
    out = pl.pallas_call(
        product_kernel,
        grid=(n // tile,),
        in_specs=[
            pl.BlockSpec((tile, m), lambda i: (i, 0)),
            pl.BlockSpec((tile, m), lambda i: (i, 0)),
            pl.BlockSpec((2 * rows, m), lambda i: (0, 0)),
            pl.BlockSpec((rows, m), lambda i: (0, 0)),
        ],
        out_specs=pl.BlockSpec((tile, rows), lambda i: (i, 0)),
        out_shape=jax.ShapeDtypeStruct((n, rows), jnp.float32),
        compiler_params=pltpu.CompilerParams(vmem_limit_bytes=48 * 1024 * 1024),
        cost_estimate=pl.CostEstimate(
            flops=6 * rows * n * m, transcendentals=0, bytes_accessed=4 * n * m + 6 * m * rows
        ),
    )(k1, k2, d12, d1)
    return out.T


def exact_dot(x, onehot, dims):
    rows = x.shape[0]
    parts = jnp.concatenate(split3(x), axis=0)
    out = lax.dot_general(parts, onehot, dims, preferred_element_type=jnp.float32)
    return (out[:rows] + out[rows:2 * rows]) + out[2 * rows:]


def solve_kernel(slot_ref, inv_ref, rcat_ref, r1_ref, o_ref):
    a = inv_ref[...]
    hi = a.astype(jnp.bfloat16)
    lo = (a - hi.astype(jnp.float32)).astype(jnp.bfloat16)
    dims = (((1,), (1,)), ((), ()))
    both = lax.dot_general(rcat_ref[...], hi, dims, preferred_element_type=jnp.float32)
    low = lax.dot_general(r1_ref[...], lo, dims, preferred_element_type=jnp.float32)
    rows = o_ref.shape[0]
    o_ref[...] = (both[:rows] + both[rows:]) + low


def solve_rows(inverse, slot, block_res, tile=512):
    _, n, width = inverse.shape
    rows = block_res.shape[0]
    r1f = lax.reduce_precision(block_res, exponent_bits=8, mantissa_bits=7)
    r1 = r1f.astype(jnp.bfloat16)
    r2 = (block_res - r1f).astype(jnp.bfloat16)
    rcat = jnp.concatenate([r1, r2], axis=0)
    tile = min(tile, n)
    grid_spec = pltpu.PrefetchScalarGridSpec(
        num_scalar_prefetch=1,
        grid=(n // tile,),
        in_specs=[
            pl.BlockSpec((None, tile, width), lambda i, s: (s[0], i, 0)),
            pl.BlockSpec((2 * rows, width), lambda i, s: (0, 0)),
            pl.BlockSpec((rows, width), lambda i, s: (0, 0)),
        ],
        out_specs=pl.BlockSpec((rows, tile), lambda i, s: (0, i)),
    )
    return pl.pallas_call(
        solve_kernel,
        grid_spec=grid_spec,
        out_shape=jax.ShapeDtypeStruct((rows, n), jnp.float32),
        compiler_params=pltpu.CompilerParams(vmem_limit_bytes=48 * 1024 * 1024),
        cost_estimate=pl.CostEstimate(
            flops=6 * rows * n * width, transcendentals=0, bytes_accessed=4 * n * width
        ),
    )(jnp.reshape(slot, (1,)).astype(jnp.int32), inverse, rcat, r1)


def body(points, residual, coef, block_of, order, inverse):
    n_grp = lax.axis_size("grp")
    n_mem = lax.axis_size("mem")
    n_dev = n_grp * n_mem
    per = B // n_dev
    slots = inverse.shape[0]
    feat = points.shape[0]
    rhs = residual.shape[0]
    mine = lax.axis_index("grp") * n_mem + lax.axis_index("mem")

    def selector(block_id):
        inside = block_of == block_id
        position = jnp.cumsum(inside.astype(jnp.int32)) - 1
        return (
            (position[:, None] == jnp.arange(per, dtype=jnp.int32)[None, :]) & inside[:, None]
        ).astype(jnp.bfloat16)

    def solve(block_res, block_id):
        return distribute(solve_rows(inverse, block_id % slots, block_res), block_id)

    def distribute(solved, block_id):
        owner = block_id // slots
        pieces = jnp.transpose(solved.reshape(rhs, n_grp, per), (1, 0, 2))
        scattered = lax.all_to_all(pieces, "grp", 0, 0, tiled=True)
        piece = lax.dynamic_index_in_dim(scattered, owner, 0, keepdims=False)
        pieces_all = gather_all(piece, n_dev)
        pieces_all = jnp.transpose(pieces_all.reshape(n_grp, n_mem, rhs, per), (2, 1, 0, 3))
        return pieces_all.reshape(rhs, B)

    def to_block(gathered, rows):
        return jnp.transpose(gathered, (1, 0, 2)).reshape(rows, B)

    block0, block1 = order[0], order[1]
    sel0 = selector(block0)
    sel1 = selector(block1)
    plain = (((1,), (0,)), ((), ()))
    chosen = exact_dot(
        jnp.concatenate([residual, points], axis=0), jnp.concatenate([sel0, sel1], axis=1), plain
    )
    chosen0 = chosen[:, :per]
    res1_start = chosen[:rhs, per:]
    pts1_local = chosen[rhs:, per:]
    gathered = to_block(gather_all(jnp.concatenate([chosen0, pts1_local], axis=0), n_dev), rhs + 2 * feat)
    block_res0 = gathered[:rhs]
    block_pts0 = gathered[rhs:rhs + feat]
    block_pts1 = gathered[rhs + feat:]

    delta0 = solve(block_res0, block0)
    owned0 = lax.dynamic_slice_in_dim(delta0, mine * per, per, axis=1)
    kernel0 = kern(points, block_pts0)
    early = apply_kernel(delta0, kern(pts1_local, block_pts0))
    overlap = lax.dot_general(sel0, sel1, (((0,), (0,)), ((), ())), preferred_element_type=jnp.float32)
    overlap = overlap.astype(jnp.bfloat16)
    res1_local = res1_start - early - ridge_weight * exact_dot(owned0, overlap, plain)
    res1_local, pts_late, pts1_late = lax.optimization_barrier((res1_local, points, block_pts1))
    block_res1 = to_block(gather_all(res1_local, n_dev), rhs)
    kernel1 = kern(pts_late, pts1_late)

    solved1 = solve_rows(inverse, block1 % slots, block_res1)
    solved1, delta0_late = lax.optimization_barrier((solved1, delta0))
    delta1 = distribute(solved1, block1)
    spread0 = exact_dot(owned0, sel0, (((1,), (1,)), ((), ())))
    update0 = apply_kernel(delta0_late, kernel0)
    residual = residual - update0 - ridge_weight * spread0
    coef = coef + spread0

    owned1 = lax.dynamic_slice_in_dim(delta1, mine * per, per, axis=1)
    spread1 = exact_dot(owned1, sel1, (((1,), (1,)), ((), ())))
    update1 = apply_kernel(delta1, kernel1)
    residual = residual - update1 - ridge_weight * spread1
    coef = coef + spread1
    return (residual, coef)


def solution(mesh):
    in_specs = (
        P(None, ("grp", "mem")),
        P(None, ("grp", "mem")),
        P(None, ("grp", "mem")),
        P(("grp", "mem")),
        P(),
        P("grp", "mem", None),
    )
    out_specs = (P(None, ("grp", "mem")), P(None, ("grp", "mem")))
    return jax.shard_map(body, mesh=mesh, in_specs=in_specs, out_specs=out_specs, check_vma=False)
```

```python
import jax
import jax.numpy as jnp
from jax import lax
from jax.sharding import PartitionSpec as P
from jax.experimental import pallas as pl
from jax.experimental.pallas import tpu as pltpu

B = 4096
STEPS = 2

ridge_weight = 0.5
kernel_scale = 0.125
ALL = ("grp", "mem")
HIGHEST = lax.Precision.HIGHEST
HIGH = lax.Precision.HIGH


def gather_all(piece, n_dev):
    sent = jnp.broadcast_to(piece[None], (n_dev,) + piece.shape)
    return lax.all_to_all(sent, ALL, 0, 0, tiled=True)


def split3(x):
    x1 = lax.reduce_precision(x, exponent_bits=8, mantissa_bits=7)
    r1 = x - x1
    x2 = lax.reduce_precision(r1, exponent_bits=8, mantissa_bits=7)
    r2 = r1 - x2
    return x1.astype(jnp.bfloat16), x2.astype(jnp.bfloat16), r2.astype(jnp.bfloat16)


def kern(u, v, keep=True):
    nu = jnp.sum(u * u, axis=0)
    nv = jnp.sum(v * v, axis=0)
    u1, u2, u3 = split3(u)
    v1, v2, v3 = split3(-2.0 * v)
    left = jnp.concatenate([u1, u1, u2, u1, u3, u2], axis=0)
    right = jnp.concatenate([v1, v2, v1, v3, v1, v2], axis=0)
    cross2 = lax.dot_general(left, right, (((0,), (0,)), ((), ())), preferred_element_type=jnp.float32)
    kernel = jnp.exp(-kernel_scale * ((nu[:, None] + nv[None, :]) + cross2))
    return lax.optimization_barrier(kernel) if keep else kernel


def apply_kernel(delta, kernel):
    return lax.dot_general(delta, kernel, (((1,), (1,)), ((), ())), precision=HIGH)


def exact_dot(x, onehot, dims):
    rows = x.shape[0]
    parts = jnp.concatenate(split3(x), axis=0)
    out = lax.dot_general(parts, onehot, dims, preferred_element_type=jnp.float32)
    return (out[:rows] + out[rows:2 * rows]) + out[2 * rows:]


def solve_kernel(slot_ref, inv_ref, rcat_ref, r1_ref, o_ref):
    a = inv_ref[...]
    hi = a.astype(jnp.bfloat16)
    lo = (a - hi.astype(jnp.float32)).astype(jnp.bfloat16)
    dims = (((1,), (1,)), ((), ()))
    both = lax.dot_general(rcat_ref[...], hi, dims, preferred_element_type=jnp.float32)
    low = lax.dot_general(r1_ref[...], lo, dims, preferred_element_type=jnp.float32)
    rows = o_ref.shape[0]
    o_ref[...] = (both[:rows] + both[rows:]) + low


def solve_rows(inverse, slot, block_res, tile=512):
    _, n, width = inverse.shape
    rows = block_res.shape[0]
    r1f = lax.reduce_precision(block_res, exponent_bits=8, mantissa_bits=7)
    r1 = r1f.astype(jnp.bfloat16)
    r2 = (block_res - r1f).astype(jnp.bfloat16)
    rcat = jnp.concatenate([r1, r2], axis=0)
    tile = min(tile, n)
    grid_spec = pltpu.PrefetchScalarGridSpec(
        num_scalar_prefetch=1,
        grid=(n // tile,),
        in_specs=[
            pl.BlockSpec((None, tile, width), lambda i, s: (s[0], i, 0)),
            pl.BlockSpec((2 * rows, width), lambda i, s: (0, 0)),
            pl.BlockSpec((rows, width), lambda i, s: (0, 0)),
        ],
        out_specs=pl.BlockSpec((rows, tile), lambda i, s: (0, i)),
    )
    return pl.pallas_call(
        solve_kernel,
        grid_spec=grid_spec,
        out_shape=jax.ShapeDtypeStruct((rows, n), jnp.float32),
        compiler_params=pltpu.CompilerParams(vmem_limit_bytes=48 * 1024 * 1024),
        cost_estimate=pl.CostEstimate(
            flops=6 * rows * n * width, transcendentals=0, bytes_accessed=4 * n * width
        ),
    )(jnp.reshape(slot, (1,)).astype(jnp.int32), inverse, rcat, r1)


def body(points, residual, coef, block_of, order, inverse):
    n_grp = lax.axis_size("grp")
    n_mem = lax.axis_size("mem")
    n_dev = n_grp * n_mem
    per = B // n_dev
    slots = inverse.shape[0]
    feat = points.shape[0]
    rhs = residual.shape[0]
    mine = lax.axis_index("grp") * n_mem + lax.axis_index("mem")

    def selector(block_id):
        inside = block_of == block_id
        position = jnp.cumsum(inside.astype(jnp.int32)) - 1
        return (
            (position[:, None] == jnp.arange(per, dtype=jnp.int32)[None, :]) & inside[:, None]
        ).astype(jnp.bfloat16)

    def solve(block_res, block_id):
        return distribute(solve_rows(inverse, block_id % slots, block_res), block_id)

    def distribute(solved, block_id):
        owner = block_id // slots
        pieces = jnp.transpose(solved.reshape(rhs, n_grp, per), (1, 0, 2))
        scattered = lax.all_to_all(pieces, "grp", 0, 0, tiled=True)
        piece = lax.dynamic_index_in_dim(scattered, owner, 0, keepdims=False)
        pieces_all = gather_all(piece, n_dev)
        pieces_all = jnp.transpose(pieces_all.reshape(n_grp, n_mem, rhs, per), (2, 1, 0, 3))
        return pieces_all.reshape(rhs, B)

    def to_block(gathered, rows):
        return jnp.transpose(gathered, (1, 0, 2)).reshape(rows, B)

    block0, block1 = order[0], order[1]
    sel0 = selector(block0)
    sel1 = selector(block1)
    plain = (((1,), (0,)), ((), ()))
    chosen = exact_dot(
        jnp.concatenate([residual, points], axis=0), jnp.concatenate([sel0, sel1], axis=1), plain
    )
    chosen0 = chosen[:, :per]
    res1_start = chosen[:rhs, per:]
    pts1_local = chosen[rhs:, per:]
    gathered = to_block(gather_all(jnp.concatenate([chosen0, pts1_local], axis=0), n_dev), rhs + 2 * feat)
    block_res0 = gathered[:rhs]
    block_pts0 = gathered[rhs:rhs + feat]
    block_pts1 = gathered[rhs + feat:]

    delta0 = solve(block_res0, block0)
    owned0 = lax.dynamic_slice_in_dim(delta0, mine * per, per, axis=1)
    kernel0 = kern(points, block_pts0)
    early = apply_kernel(delta0, kern(pts1_local, block_pts0, keep=False))
    overlap = lax.dot_general(sel0, sel1, (((0,), (0,)), ((), ())), preferred_element_type=jnp.float32)
    overlap = overlap.astype(jnp.bfloat16)
    res1_local = res1_start - early - ridge_weight * exact_dot(owned0, overlap, plain)
    res1_local, pts_late, pts1_late = lax.optimization_barrier((res1_local, points, block_pts1))
    block_res1 = to_block(gather_all(res1_local, n_dev), rhs)
    kernel1 = kern(pts_late, pts1_late)

    solved1 = solve_rows(inverse, block1 % slots, block_res1)
    solved1, delta0_late = lax.optimization_barrier((solved1, delta0))
    delta1 = distribute(solved1, block1)
    spread0 = exact_dot(owned0, sel0, (((1,), (1,)), ((), ())))
    update0 = apply_kernel(delta0_late, kernel0)
    residual = residual - update0 - ridge_weight * spread0
    coef = coef + spread0

    owned1 = lax.dynamic_slice_in_dim(delta1, mine * per, per, axis=1)
    spread1 = exact_dot(owned1, sel1, (((1,), (1,)), ((), ())))
    update1 = apply_kernel(delta1, kernel1)
    residual = residual - update1 - ridge_weight * spread1
    coef = coef + spread1
    return (residual, coef)


def solution(mesh):
    in_specs = (
        P(None, ("grp", "mem")),
        P(None, ("grp", "mem")),
        P(None, ("grp", "mem")),
        P(("grp", "mem")),
        P(),
        P("grp", "mem", None),
    )
    out_specs = (P(None, ("grp", "mem")), P(None, ("grp", "mem")))
    return jax.shard_map(body, mesh=mesh, in_specs=in_specs, out_specs=out_specs, check_vma=False)
```

```python
import jax
import jax.numpy as jnp
from jax import lax
from jax.sharding import PartitionSpec as P
from jax.experimental import pallas as pl
from jax.experimental.pallas import tpu as pltpu

B = 4096
STEPS = 2

ridge_weight = 0.5
kernel_scale = 0.125
ALL = ("grp", "mem")
HIGHEST = lax.Precision.HIGHEST
HIGH = lax.Precision.HIGH


def gather_all(piece, n_dev):
    sent = jnp.broadcast_to(piece[None], (n_dev,) + piece.shape)
    return lax.all_to_all(sent, ALL, 0, 0, tiled=True)


def split3(x):
    x1 = lax.reduce_precision(x, exponent_bits=8, mantissa_bits=7)
    r1 = x - x1
    x2 = lax.reduce_precision(r1, exponent_bits=8, mantissa_bits=7)
    r2 = r1 - x2
    return x1.astype(jnp.bfloat16), x2.astype(jnp.bfloat16), r2.astype(jnp.bfloat16)


def kern(u, v, keep=True):
    nu = jnp.sum(u * u, axis=0)
    nv = jnp.sum(v * v, axis=0)
    u1, u2, u3 = split3(u)
    v1, v2, v3 = split3(-2.0 * v)
    left = jnp.concatenate([u1, u1, u2, u1, u3, u2], axis=0)
    right = jnp.concatenate([v1, v2, v1, v3, v1, v2], axis=0)
    cross2 = lax.dot_general(left, right, (((0,), (0,)), ((), ())), preferred_element_type=jnp.float32)
    kernel = jnp.exp(-kernel_scale * ((nu[:, None] + nv[None, :]) + cross2))
    return lax.optimization_barrier(kernel) if keep else kernel


def apply_kernel(delta, kernel):
    return lax.dot_general(delta, kernel, (((1,), (1,)), ((), ())), precision=HIGH)


def exact_dot(x, onehot, dims):
    rows = x.shape[0]
    parts = jnp.concatenate(split3(x), axis=0)
    out = lax.dot_general(parts, onehot, dims, preferred_element_type=jnp.float32)
    return (out[:rows] + out[rows:2 * rows]) + out[2 * rows:]


def solve_kernel(slot_ref, inv_ref, rcat_ref, r1_ref, o_ref):
    a = inv_ref[...]
    hi = a.astype(jnp.bfloat16)
    lo = (a - hi.astype(jnp.float32)).astype(jnp.bfloat16)
    dims = (((1,), (1,)), ((), ()))
    both = lax.dot_general(rcat_ref[...], hi, dims, preferred_element_type=jnp.float32)
    low = lax.dot_general(r1_ref[...], lo, dims, preferred_element_type=jnp.float32)
    rows = o_ref.shape[0]
    o_ref[...] = (both[:rows] + both[rows:]) + low


def solve_rows(inverse, slot, block_res, tile=512):
    _, n, width = inverse.shape
    rows = block_res.shape[0]
    r1f = lax.reduce_precision(block_res, exponent_bits=8, mantissa_bits=7)
    r1 = r1f.astype(jnp.bfloat16)
    r2 = (block_res - r1f).astype(jnp.bfloat16)
    rcat = jnp.concatenate([r1, r2], axis=0)
    tile = min(tile, n)
    grid_spec = pltpu.PrefetchScalarGridSpec(
        num_scalar_prefetch=1,
        grid=(n // tile,),
        in_specs=[
            pl.BlockSpec((None, tile, width), lambda i, s: (s[0], i, 0)),
            pl.BlockSpec((2 * rows, width), lambda i, s: (0, 0)),
            pl.BlockSpec((rows, width), lambda i, s: (0, 0)),
        ],
        out_specs=pl.BlockSpec((rows, tile), lambda i, s: (0, i)),
    )
    return pl.pallas_call(
        solve_kernel,
        grid_spec=grid_spec,
        out_shape=jax.ShapeDtypeStruct((rows, n), jnp.float32),
        compiler_params=pltpu.CompilerParams(vmem_limit_bytes=48 * 1024 * 1024),
        cost_estimate=pl.CostEstimate(
            flops=6 * rows * n * width, transcendentals=0, bytes_accessed=4 * n * width
        ),
    )(jnp.reshape(slot, (1,)).astype(jnp.int32), inverse, rcat, r1)


def body(points, residual, coef, block_of, order, inverse):
    n_grp = lax.axis_size("grp")
    n_mem = lax.axis_size("mem")
    n_dev = n_grp * n_mem
    per = B // n_dev
    slots = inverse.shape[0]
    feat = points.shape[0]
    rhs = residual.shape[0]
    mine = lax.axis_index("grp") * n_mem + lax.axis_index("mem")

    def selector(block_id):
        inside = block_of == block_id
        position = jnp.cumsum(inside.astype(jnp.int32)) - 1
        return (
            (position[:, None] == jnp.arange(per, dtype=jnp.int32)[None, :]) & inside[:, None]
        ).astype(jnp.bfloat16)

    def solve(block_res, block_id):
        return distribute(solve_rows(inverse, block_id % slots, block_res), block_id)

    def distribute(solved, block_id):
        owner = block_id // slots
        pieces = jnp.transpose(solved.reshape(rhs, n_grp, per), (1, 0, 2))
        scattered = lax.all_to_all(pieces, "grp", 0, 0, tiled=True)
        piece = lax.dynamic_index_in_dim(scattered, owner, 0, keepdims=False)
        pieces_all = gather_all(piece, n_dev)
        pieces_all = jnp.transpose(pieces_all.reshape(n_grp, n_mem, rhs, per), (2, 1, 0, 3))
        return pieces_all.reshape(rhs, B)

    def to_block(gathered, rows):
        return jnp.transpose(gathered, (1, 0, 2)).reshape(rows, B)

    block0, block1 = order[0], order[1]
    sel0 = selector(block0)
    sel1 = selector(block1)
    plain = (((1,), (0,)), ((), ()))
    chosen = exact_dot(
        jnp.concatenate([residual, points], axis=0), jnp.concatenate([sel0, sel1], axis=1), plain
    )
    chosen0 = chosen[:, :per]
    res1_start = chosen[:rhs, per:]
    pts1_local = chosen[rhs:, per:]
    gathered = to_block(gather_all(jnp.concatenate([chosen0, pts1_local], axis=0), n_dev), rhs + 2 * feat)
    block_res0 = gathered[:rhs]
    block_pts0 = gathered[rhs:rhs + feat]
    block_pts1 = gathered[rhs + feat:]

    delta0 = solve(block_res0, block0)
    owned0 = lax.dynamic_slice_in_dim(delta0, mine * per, per, axis=1)
    kernel0 = kern(points, block_pts0)
    early = apply_kernel(delta0, kern(pts1_local, block_pts0, keep=False))
    overlap = lax.dot_general(sel0, sel1, (((0,), (0,)), ((), ())), preferred_element_type=jnp.float32)
    overlap = overlap.astype(jnp.bfloat16)
    wide = lambda x: jnp.broadcast_to(x[None], (n_dev,) + x.shape)
    sent1 = wide(res1_start) - wide(early) - ridge_weight * wide(exact_dot(owned0, overlap, plain))
    res1_local = sent1[0]
    sent1, pts_late, pts1_late = lax.optimization_barrier((sent1, points, block_pts1))
    block_res1 = to_block(lax.all_to_all(sent1, ALL, 0, 0, tiled=True), rhs)
    kernel1 = kern(pts_late, pts1_late)

    solved1 = solve_rows(inverse, block1 % slots, block_res1)
    solved1, delta0_late = lax.optimization_barrier((solved1, delta0))
    delta1 = distribute(solved1, block1)
    spread0 = exact_dot(owned0, sel0, (((1,), (1,)), ((), ())))
    update0 = apply_kernel(delta0_late, kernel0)
    residual = residual - update0 - ridge_weight * spread0
    coef = coef + spread0

    owned1 = lax.dynamic_slice_in_dim(delta1, mine * per, per, axis=1)
    spread1 = exact_dot(owned1, sel1, (((1,), (1,)), ((), ())))
    update1 = apply_kernel(delta1, kernel1)
    residual = residual - update1 - ridge_weight * spread1
    coef = coef + spread1
    return (residual, coef)


def solution(mesh):
    in_specs = (
        P(None, ("grp", "mem")),
        P(None, ("grp", "mem")),
        P(None, ("grp", "mem")),
        P(("grp", "mem")),
        P(),
        P("grp", "mem", None),
    )
    out_specs = (P(None, ("grp", "mem")), P(None, ("grp", "mem")))
    return jax.shard_map(body, mesh=mesh, in_specs=in_specs, out_specs=out_specs, check_vma=False)
```

```python
import jax
import jax.numpy as jnp
from jax import lax
from jax.sharding import PartitionSpec as P
from jax.experimental import pallas as pl
from jax.experimental.pallas import tpu as pltpu

B = 4096
STEPS = 2

ridge_weight = 0.5
kernel_scale = 0.125
ALL = ("grp", "mem")
HIGHEST = lax.Precision.HIGHEST
HIGH = lax.Precision.HIGH


def gather_all(piece, n_dev):
    sent = jnp.broadcast_to(piece[None], (n_dev,) + piece.shape)
    return lax.all_to_all(sent, ALL, 0, 0, tiled=True)


def split3(x):
    x1 = lax.reduce_precision(x, exponent_bits=8, mantissa_bits=7)
    r1 = x - x1
    x2 = lax.reduce_precision(r1, exponent_bits=8, mantissa_bits=7)
    r2 = r1 - x2
    return x1.astype(jnp.bfloat16), x2.astype(jnp.bfloat16), r2.astype(jnp.bfloat16)


def kern(u, v, keep=True):
    nu = jnp.sum(u * u, axis=0)
    nv = jnp.sum(v * v, axis=0)
    u1, u2, u3 = split3(u)
    v1, v2, v3 = split3(-2.0 * v)
    left = jnp.concatenate([u1, u1, u2, u1, u3, u2], axis=0)
    right = jnp.concatenate([v1, v2, v1, v3, v1, v2], axis=0)
    cross2 = lax.dot_general(left, right, (((0,), (0,)), ((), ())), preferred_element_type=jnp.float32)
    kernel = jnp.exp(-kernel_scale * ((nu[:, None] + nv[None, :]) + cross2))
    return lax.optimization_barrier(kernel) if keep else kernel


def apply_kernel(delta, kernel):
    return lax.dot_general(delta, kernel, (((1,), (1,)), ((), ())), precision=HIGH)


def exact_dot(x, onehot, dims):
    rows = x.shape[0]
    parts = jnp.concatenate(split3(x), axis=0)
    out = lax.dot_general(parts, onehot, dims, preferred_element_type=jnp.float32)
    return (out[:rows] + out[rows:2 * rows]) + out[2 * rows:]


def solve_kernel(slot_ref, inv_ref, rcat_ref, r1_ref, o_ref):
    a = inv_ref[...]
    hi = a.astype(jnp.bfloat16)
    lo = (a - hi.astype(jnp.float32)).astype(jnp.bfloat16)
    dims = (((1,), (1,)), ((), ()))
    both = lax.dot_general(rcat_ref[...], hi, dims, preferred_element_type=jnp.float32)
    low = lax.dot_general(r1_ref[...], lo, dims, preferred_element_type=jnp.float32)
    rows = o_ref.shape[0]
    o_ref[...] = (both[:rows] + both[rows:]) + low


def solve_rows(inverse, slot, block_res, tile=512):
    _, n, width = inverse.shape
    rows = block_res.shape[0]
    r1f = lax.reduce_precision(block_res, exponent_bits=8, mantissa_bits=7)
    r1 = r1f.astype(jnp.bfloat16)
    r2 = (block_res - r1f).astype(jnp.bfloat16)
    rcat = jnp.concatenate([r1, r2], axis=0)
    tile = min(tile, n)
    grid_spec = pltpu.PrefetchScalarGridSpec(
        num_scalar_prefetch=1,
        grid=(n // tile,),
        in_specs=[
            pl.BlockSpec((None, tile, width), lambda i, s: (s[0], i, 0)),
            pl.BlockSpec((2 * rows, width), lambda i, s: (0, 0)),
            pl.BlockSpec((rows, width), lambda i, s: (0, 0)),
        ],
        out_specs=pl.BlockSpec((rows, tile), lambda i, s: (0, i)),
    )
    return pl.pallas_call(
        solve_kernel,
        grid_spec=grid_spec,
        out_shape=jax.ShapeDtypeStruct((rows, n), jnp.float32),
        compiler_params=pltpu.CompilerParams(vmem_limit_bytes=48 * 1024 * 1024),
        cost_estimate=pl.CostEstimate(
            flops=6 * rows * n * width, transcendentals=0, bytes_accessed=4 * n * width
        ),
    )(jnp.reshape(slot, (1,)).astype(jnp.int32), inverse, rcat, r1)


def body(points, residual, coef, block_of, order, inverse):
    n_grp = lax.axis_size("grp")
    n_mem = lax.axis_size("mem")
    n_dev = n_grp * n_mem
    per = B // n_dev
    slots = inverse.shape[0]
    feat = points.shape[0]
    rhs = residual.shape[0]
    mine = lax.axis_index("grp") * n_mem + lax.axis_index("mem")

    def selector(block_id):
        inside = block_of == block_id
        position = jnp.cumsum(inside.astype(jnp.int32)) - 1
        return (
            (position[:, None] == jnp.arange(per, dtype=jnp.int32)[None, :]) & inside[:, None]
        ).astype(jnp.bfloat16)

    def solve(block_res, block_id):
        return distribute(solve_rows(inverse, block_id % slots, block_res), block_id)

    def distribute(solved, block_id):
        owner = block_id // slots
        pieces = jnp.transpose(solved.reshape(rhs, n_grp, per), (1, 0, 2))
        scattered = lax.all_to_all(pieces, "grp", 0, 0, tiled=True)
        piece = lax.dynamic_index_in_dim(scattered, owner, 0, keepdims=False)
        pieces_all = gather_all(piece, n_dev)
        pieces_all = jnp.transpose(pieces_all.reshape(n_grp, n_mem, rhs, per), (2, 1, 0, 3))
        return pieces_all.reshape(rhs, B)

    def to_block(gathered, rows):
        return jnp.transpose(gathered, (1, 0, 2)).reshape(rows, B)

    block0, block1 = order[0], order[1]
    sel0 = selector(block0)
    sel1 = selector(block1)
    plain = (((1,), (0,)), ((), ()))
    chosen = exact_dot(
        jnp.concatenate([residual, points], axis=0), jnp.concatenate([sel0, sel1], axis=1), plain
    )
    chosen0 = chosen[:, :per]
    res1_start = chosen[:rhs, per:]
    pts1_local = chosen[rhs:, per:]
    src = jnp.concatenate(split3(jnp.concatenate([residual, points], axis=0)), axis=0)
    partial = lax.dot_general(src, jnp.concatenate([sel0, sel1], axis=1), plain, preferred_element_type=jnp.float32)
    rows_src = rhs + feat
    wide = lambda x: jnp.broadcast_to(x[None], (n_dev,) + x.shape)
    terms = [partial[k * rows_src:(k + 1) * rows_src] for k in range(3)]
    terms = [wide(jnp.concatenate([t[:, :per], t[rhs:, per:]], axis=0)) for t in terms]
    sent0 = (terms[0] + terms[1]) + terms[2]
    gathered = to_block(lax.all_to_all(sent0, ALL, 0, 0, tiled=True), rhs + 2 * feat)
    block_res0 = gathered[:rhs]
    block_pts0 = gathered[rhs:rhs + feat]
    block_pts1 = gathered[rhs + feat:]

    delta0 = solve(block_res0, block0)
    owned0 = lax.dynamic_slice_in_dim(delta0, mine * per, per, axis=1)
    kernel0 = kern(points, block_pts0)
    early = apply_kernel(delta0, kern(pts1_local, block_pts0, keep=False))
    overlap = lax.dot_general(sel0, sel1, (((0,), (0,)), ((), ())), preferred_element_type=jnp.float32)
    overlap = overlap.astype(jnp.bfloat16)
    wide = lambda x: jnp.broadcast_to(x[None], (n_dev,) + x.shape)
    sent1 = wide(res1_start) - wide(early) - ridge_weight * wide(exact_dot(owned0, overlap, plain))
    res1_local = sent1[0]
    sent1, pts_late, pts1_late = lax.optimization_barrier((sent1, points, block_pts1))
    block_res1 = to_block(lax.all_to_all(sent1, ALL, 0, 0, tiled=True), rhs)
    kernel1 = kern(pts_late, pts1_late)

    solved1 = solve_rows(inverse, block1 % slots, block_res1)
    solved1, delta0_late = lax.optimization_barrier((solved1, delta0))
    delta1 = distribute(solved1, block1)
    spread0 = exact_dot(owned0, sel0, (((1,), (1,)), ((), ())))
    update0 = apply_kernel(delta0_late, kernel0)
    residual = residual - update0 - ridge_weight * spread0
    coef = coef + spread0

    owned1 = lax.dynamic_slice_in_dim(delta1, mine * per, per, axis=1)
    spread1 = exact_dot(owned1, sel1, (((1,), (1,)), ((), ())))
    update1 = apply_kernel(delta1, kernel1)
    residual = residual - update1 - ridge_weight * spread1
    coef = coef + spread1
    return (residual, coef)


def solution(mesh):
    in_specs = (
        P(None, ("grp", "mem")),
        P(None, ("grp", "mem")),
        P(None, ("grp", "mem")),
        P(("grp", "mem")),
        P(),
        P("grp", "mem", None),
    )
    out_specs = (P(None, ("grp", "mem")), P(None, ("grp", "mem")))
    return jax.shard_map(body, mesh=mesh, in_specs=in_specs, out_specs=out_specs, check_vma=False)
```

```python
import jax
import jax.numpy as jnp
from jax import lax
from jax.sharding import PartitionSpec as P
from jax.experimental import pallas as pl
from jax.experimental.pallas import tpu as pltpu

B = 4096
STEPS = 2

ridge_weight = 0.5
kernel_scale = 0.125
ALL = ("grp", "mem")
HIGHEST = lax.Precision.HIGHEST
HIGH = lax.Precision.HIGH


def gather_all(piece, n_dev):
    sent = jnp.broadcast_to(piece[None], (n_dev,) + piece.shape)
    return lax.all_to_all(sent, ALL, 0, 0, tiled=True)


def split3(x):
    x1 = lax.reduce_precision(x, exponent_bits=8, mantissa_bits=7)
    r1 = x - x1
    x2 = lax.reduce_precision(r1, exponent_bits=8, mantissa_bits=7)
    r2 = r1 - x2
    return x1.astype(jnp.bfloat16), x2.astype(jnp.bfloat16), r2.astype(jnp.bfloat16)


def kern(u, v, keep=True):
    nu = jnp.sum(u * u, axis=0)
    nv = jnp.sum(v * v, axis=0)
    u1, u2, u3 = split3(u)
    v1, v2, v3 = split3(-2.0 * v)
    left = jnp.concatenate([u1, u1, u2, u1, u3, u2], axis=0)
    right = jnp.concatenate([v1, v2, v1, v3, v1, v2], axis=0)
    cross2 = lax.dot_general(left, right, (((0,), (0,)), ((), ())), preferred_element_type=jnp.float32)
    kernel = jnp.exp(-kernel_scale * ((nu[:, None] + nv[None, :]) + cross2))
    return lax.optimization_barrier(kernel) if keep else kernel


def apply_kernel(delta, kernel):
    return lax.dot_general(delta, kernel, (((1,), (1,)), ((), ())), precision=HIGH)


def exact_dot(x, onehot, dims):
    rows = x.shape[0]
    parts = jnp.concatenate(split3(x), axis=0)
    out = lax.dot_general(parts, onehot, dims, preferred_element_type=jnp.float32)
    return (out[:rows] + out[rows:2 * rows]) + out[2 * rows:]


def solve_kernel(slot_ref, inv_ref, rcat_ref, r1_ref, o_ref):
    a = inv_ref[...]
    hi = a.astype(jnp.bfloat16)
    lo = (a - hi.astype(jnp.float32)).astype(jnp.bfloat16)
    dims = (((1,), (1,)), ((), ()))
    both = lax.dot_general(rcat_ref[...], hi, dims, preferred_element_type=jnp.float32)
    low = lax.dot_general(r1_ref[...], lo, dims, preferred_element_type=jnp.float32)
    rows = o_ref.shape[0]
    o_ref[...] = (both[:rows] + both[rows:]) + low


def solve_rows(inverse, slot, block_res, tile=512):
    _, n, width = inverse.shape
    rows = block_res.shape[0]
    r1f = lax.reduce_precision(block_res, exponent_bits=8, mantissa_bits=7)
    r1 = r1f.astype(jnp.bfloat16)
    r2 = (block_res - r1f).astype(jnp.bfloat16)
    rcat = jnp.concatenate([r1, r2], axis=0)
    tile = min(tile, n)
    grid_spec = pltpu.PrefetchScalarGridSpec(
        num_scalar_prefetch=1,
        grid=(n // tile,),
        in_specs=[
            pl.BlockSpec((None, tile, width), lambda i, s: (s[0], i, 0)),
            pl.BlockSpec((2 * rows, width), lambda i, s: (0, 0)),
            pl.BlockSpec((rows, width), lambda i, s: (0, 0)),
        ],
        out_specs=pl.BlockSpec((rows, tile), lambda i, s: (0, i)),
    )
    return pl.pallas_call(
        solve_kernel,
        grid_spec=grid_spec,
        out_shape=jax.ShapeDtypeStruct((rows, n), jnp.float32),
        compiler_params=pltpu.CompilerParams(vmem_limit_bytes=48 * 1024 * 1024),
        cost_estimate=pl.CostEstimate(
            flops=6 * rows * n * width, transcendentals=0, bytes_accessed=4 * n * width
        ),
    )(jnp.reshape(slot, (1,)).astype(jnp.int32), inverse, rcat, r1)


def body(points, residual, coef, block_of, order, inverse):
    n_grp = lax.axis_size("grp")
    n_mem = lax.axis_size("mem")
    n_dev = n_grp * n_mem
    per = B // n_dev
    slots = inverse.shape[0]
    feat = points.shape[0]
    rhs = residual.shape[0]
    mine = lax.axis_index("grp") * n_mem + lax.axis_index("mem")

    def selector(block_id):
        inside = block_of == block_id
        position = jnp.cumsum(inside.astype(jnp.int32)) - 1
        return (
            (position[:, None] == jnp.arange(per, dtype=jnp.int32)[None, :]) & inside[:, None]
        ).astype(jnp.bfloat16)

    def solve(block_res, block_id):
        return distribute(solve_rows(inverse, block_id % slots, block_res), block_id)

    def distribute(solved, block_id):
        owner = block_id // slots
        pieces = jnp.transpose(solved.reshape(rhs, n_grp, per), (1, 0, 2))
        scattered = lax.all_to_all(pieces, "grp", 0, 0, tiled=True)
        sent = scattered[jnp.full((n_dev,), owner, dtype=jnp.int32)]
        pieces_all = lax.all_to_all(sent, ALL, 0, 0, tiled=True)
        pieces_all = jnp.transpose(pieces_all.reshape(n_grp, n_mem, rhs, per), (2, 1, 0, 3))
        return pieces_all.reshape(rhs, B)

    def to_block(gathered, rows):
        return jnp.transpose(gathered, (1, 0, 2)).reshape(rows, B)

    block0, block1 = order[0], order[1]
    sel0 = selector(block0)
    sel1 = selector(block1)
    plain = (((1,), (0,)), ((), ()))
    chosen = exact_dot(
        jnp.concatenate([residual, points], axis=0), jnp.concatenate([sel0, sel1], axis=1), plain
    )
    chosen0 = chosen[:, :per]
    res1_start = chosen[:rhs, per:]
    pts1_local = chosen[rhs:, per:]
    src = jnp.concatenate(split3(jnp.concatenate([residual, points], axis=0)), axis=0)
    partial = lax.dot_general(src, jnp.concatenate([sel0, sel1], axis=1), plain, preferred_element_type=jnp.float32)
    rows_src = rhs + feat
    wide = lambda x: jnp.broadcast_to(x[None], (n_dev,) + x.shape)
    terms = [partial[k * rows_src:(k + 1) * rows_src] for k in range(3)]
    terms = [wide(jnp.concatenate([t[:, :per], t[rhs:, per:]], axis=0)) for t in terms]
    sent0 = (terms[0] + terms[1]) + terms[2]
    gathered = to_block(lax.all_to_all(sent0, ALL, 0, 0, tiled=True), rhs + 2 * feat)
    block_res0 = gathered[:rhs]
    block_pts0 = gathered[rhs:rhs + feat]
    block_pts1 = gathered[rhs + feat:]

    delta0 = solve(block_res0, block0)
    owned0 = lax.dynamic_slice_in_dim(delta0, mine * per, per, axis=1)
    kernel0 = kern(points, block_pts0)
    early = apply_kernel(delta0, kern(pts1_local, block_pts0, keep=False))
    overlap = lax.dot_general(sel0, sel1, (((0,), (0,)), ((), ())), preferred_element_type=jnp.float32)
    overlap = overlap.astype(jnp.bfloat16)
    wide = lambda x: jnp.broadcast_to(x[None], (n_dev,) + x.shape)
    sent1 = wide(res1_start) - wide(early) - ridge_weight * wide(exact_dot(owned0, overlap, plain))
    res1_local = sent1[0]
    sent1, pts_late, pts1_late = lax.optimization_barrier((sent1, points, block_pts1))
    block_res1 = to_block(lax.all_to_all(sent1, ALL, 0, 0, tiled=True), rhs)
    kernel1 = kern(pts_late, pts1_late)

    solved1 = solve_rows(inverse, block1 % slots, block_res1)
    solved1, delta0_late = lax.optimization_barrier((solved1, delta0))
    delta1 = distribute(solved1, block1)
    spread0 = exact_dot(owned0, sel0, (((1,), (1,)), ((), ())))
    update0 = apply_kernel(delta0_late, kernel0)
    residual = residual - update0 - ridge_weight * spread0
    coef = coef + spread0

    owned1 = lax.dynamic_slice_in_dim(delta1, mine * per, per, axis=1)
    spread1 = exact_dot(owned1, sel1, (((1,), (1,)), ((), ())))
    update1 = apply_kernel(delta1, kernel1)
    residual = residual - update1 - ridge_weight * spread1
    coef = coef + spread1
    return (residual, coef)


def solution(mesh):
    in_specs = (
        P(None, ("grp", "mem")),
        P(None, ("grp", "mem")),
        P(None, ("grp", "mem")),
        P(("grp", "mem")),
        P(),
        P("grp", "mem", None),
    )
    out_specs = (P(None, ("grp", "mem")), P(None, ("grp", "mem")))
    return jax.shard_map(body, mesh=mesh, in_specs=in_specs, out_specs=out_specs, check_vma=False)
```
